256 devices in a mesh: outer: 4 (over y_hi, core), dp: 4 (over x), mp: 16 (over z, y_lo).
Axes of the slice: x: 4, y: 4 (y_hi: 2, y_lo: 2; y = y_hi * 2 + y_lo), z: 8, core: 2. Of those that a mesh axis runs over, the one named last changes fastest.
Arguments:
- tokens: bfloat16 [4, 4096, 2048], P('outer', 'dp'), may hold values from -6 to 6
- cotangent: bfloat16 [4, 4096, 2048], P('outer', 'dp'), may hold values from -0.59765625 to 0.59765625
- gate_weight: bfloat16 [4, 2048, 6144], P('outer', 'dp', 'mp'), may hold values from -0.125 to 0.125
- up_weight: bfloat16 [4, 2048, 6144], P('outer', 'dp', 'mp'), may hold values from -0.125 to 0.125
- down_master: float32 [4, 6144, 2048], P('outer', 'mp', 'dp'), may hold values from -0.0375 to 0.0375
- first_moment: float32 [4, 6144, 2048], P('outer', 'mp', 'dp'), may hold values from -0.6 to 0.6
- second_moment: float32 [4, 6144, 2048], P('outer', 'mp', 'dp'), may hold values from 1 to 10
- anchor: float32 [6144, 2048], P('mp', 'dp'), may hold values from -0.0375 to 0.0375
- outer_momentum: float32 [6144, 2048], P('mp', 'dp'), may hold values from -0.00018 to 0.00018
Outputs:
- new_params: float32 [6144, 2048], P('mp', 'dp')
- first_out: float32 [4, 6144, 2048], P('outer', 'mp', 'dp')
- second_out: float32 [4, 6144, 2048], P('outer', 'mp', 'dp')
- momentum_out: float32 [6144, 2048], P('mp', 'dp')
- input_grad: bfloat16 [4, 4096, 2048], P('outer', ('dp', 'mp'))
The draws below stay inside these ranges and needn't reach their ends.
All inputs are finite; a program needn't handle non-finite values.
Results may differ from the reference program's by a relative error of at most 0.023.
Values may be sent and summed in bfloat16 or wider, within the bound.
No kernel may reach another device: no remote copies, remote signals or barrier semaphores. Data moves between devices by JAX's collectives and lax.ppermute only.
A program may use at most 128 MiB of HBM per device.

```python
import math
import jax
import jax.numpy as jnp

D = 2048
FF = 6144
TOKENS = 4096
REPLICAS = 4
N_OUTER = 4
N_MP = 16


def base_field(key):
    values = jax.random.normal(jax.random.fold_in(key, 17), (FF, D), jnp.float32)
    return 0.0125 * jnp.clip(values, -3.0, 3.0)


def draw_anchor(key, part):
    return base_field(key)


def draw_down_master(key, part):
    wander = 1e-05 * jax.random.normal(jax.random.fold_in(key, 29), (REPLICAS, FF, D), jnp.float32)
    return jnp.clip(base_field(key)[None] + wander, -0.0375, 0.0375)


def level_of(rng, shape, cuts, smallest, high):
    def one(axis_at, parts):
        draws = jax.random.uniform(jax.random.fold_in(jax.random.fold_in(rng, 6), axis_at), (parts,), jnp.float32, smallest / len(cuts), high / len(cuts))
        return jnp.repeat(jnp.exp(draws), shape[axis_at] // parts).reshape((-1,) + (1,) * (len(shape) - axis_at - 1))

    level = one(*cuts[0])
    for cut in cuts[1:]:
        level = level * one(*cut)
    return level


def centred(stream_key, extent, width, limit, pieces=(), dtype=jnp.bfloat16):
    entries = width * jax.random.normal(stream_key, extent, jnp.float32)
    if pieces:
        entries = entries * level_of(stream_key, extent, pieces, -0.22, 0.18)
    return jnp.clip(entries, -limit, limit).astype(dtype)


def setup_inputs(seed: int = 0) -> dict:
    keys = jax.random.split(jax.random.key(seed), 10)
    return {
        "tokens": centred(keys[0], (REPLICAS, TOKENS, D), 1.0, 6.0, ((0, 4), (1, 4))),
        "cotangent": centred(keys[1], (REPLICAS, TOKENS, D), 0.1, 0.59765625, ((0, 4), (1, 4))),
        "gate_weight": centred(keys[2], (REPLICAS, D, FF), D ** -0.5, 0.125, ((0, 4), (1, 4), (2, 16))),
        "up_weight": centred(keys[3], (REPLICAS, D, FF), D ** -0.5, 0.125, ((0, 4), (1, 4), (2, 16))),
        "down_master": draw_down_master(jax.random.fold_in(keys[9], 71), 0),
        "first_moment": centred(keys[5], (REPLICAS, FF, D), 0.1, 0.6, ((0, 4), (1, 16), (2, 4)), jnp.float32),
        "second_moment": jnp.clip(jnp.exp(math.log(10.0) - 2.3025851 * jax.random.uniform(keys[6], (REPLICAS, FF, D), jnp.float32) ** level_of(keys[6], (REPLICAS, FF, D), ((0, 4), (1, 16), (2, 4)), -0.2, 0.2)), 1.0, 10.0),
        "anchor": draw_anchor(jax.random.fold_in(keys[9], 71), 0),
        "outer_momentum": centred(keys[8], (FF, D), 0.00003, 0.00018, ((0, 16), (1, 4)), jnp.float32),
    }


bias_one = 1.0 - (0.9 ** 50) ** 2
bias_two = 1.0 - (0.999 ** 50) ** 2

def replica_drift(inputs, upstream, gate_w, up_w, master, moment_one, moment_two, anchor):
    gate_pre = jnp.dot(inputs, gate_w, preferred_element_type=jnp.float32)
    up_pre = jnp.dot(inputs, up_w, preferred_element_type=jnp.float32)
    gate_sigmoid = jax.nn.sigmoid(gate_pre)
    active = gate_pre * gate_sigmoid
    hidden = (active * up_pre).astype(jnp.bfloat16)
    down_half = master.astype(jnp.bfloat16)
    grad_hidden = jnp.dot(upstream, down_half.T, preferred_element_type=jnp.float32)
    grad_up = (grad_hidden * active).astype(jnp.bfloat16)
    grad_gate = (grad_hidden * up_pre * gate_sigmoid * (1.0 + gate_pre * (1.0 - gate_sigmoid))).astype(jnp.bfloat16)
    block_width = FF // N_MP
    summed = jnp.zeros((inputs.shape[0], inputs.shape[1]), jnp.float32)
    for block_idx in range(N_MP):
        lower = block_idx * block_width
        upper = lower + block_width
        partial_term = jnp.dot(grad_gate[:, lower:upper], gate_w[:, lower:upper].T, preferred_element_type=jnp.float32)
        partial_term = partial_term + jnp.dot(grad_up[:, lower:upper], up_w[:, lower:upper].T, preferred_element_type=jnp.float32)
        summed = summed + partial_term.astype(jnp.bfloat16).astype(jnp.float32)
    input_grad = summed.astype(jnp.bfloat16)
    grad_down = jnp.dot(hidden.T, upstream, preferred_element_type=jnp.float32)
    first_new = 0.9 * moment_one + 0.1 * grad_down
    second_new = 0.999 * moment_two + 0.001 * grad_down * grad_down
    adam_step = first_new / bias_one / (jnp.sqrt(second_new / bias_two) + 1e-08) + 0.1 * master
    inner_params = master - 0.001 * adam_step
    return (anchor - inner_params, first_new, second_new, input_grad)

def reference(tokens, cotangent, gate_weight, up_weight, down_master, first_moment, second_moment, anchor, outer_momentum):
    drift_total = jnp.zeros(anchor.shape, jnp.float32)
    firsts = []
    seconds = []
    grads = []
    for replica in range(N_OUTER):
        drift_local, first_new, second_new, input_grad = replica_drift(tokens[replica], cotangent[replica], gate_weight[replica], up_weight[replica], down_master[replica], first_moment[replica], second_moment[replica], anchor)
        drift_total = drift_total + drift_local
        firsts.append(first_new)
        seconds.append(second_new)
        grads.append(input_grad)
    mean_drift = drift_total / N_OUTER
    momentum_out = 0.9 * outer_momentum + mean_drift
    new_params = anchor - 0.7 * (mean_drift + 0.9 * momentum_out)
    return (new_params, jnp.stack(firsts), jnp.stack(seconds), momentum_out, jnp.stack(grads))
```

```python
import jax
import jax.numpy as jnp
from jax import lax
from jax.sharding import PartitionSpec as P

bias_one = 1.0 - (0.9**50) ** 2
bias_two = 1.0 - (0.999**50) ** 2


def _shift(n, s):
    return [(i, (i + s) % n) for i in range(n)]


def shards(
    tokens,
    cotangent,
    gate_weight,
    up_weight,
    down_master,
    first_moment,
    second_moment,
    anchor,
    outer_momentum,
):
    ndp = lax.axis_size("dp")
    j = lax.axis_index("dp")
    inputs = tokens[0]
    upstream = cotangent[0]
    master = down_master[0]
    down_half = master.astype(jnp.bfloat16)
    ff = master.shape[0]

    shard = jnp.concatenate([gate_weight[0], up_weight[0], down_half.T], axis=1)
    rows = shard.shape[0]
    half = rows // 2
    a, b = shard[:half], shard[half:]
    pieces = [(j, 0, a), (j, 1, b)]
    for s in range(1, ndp):
        a = lax.ppermute(a, "dp", _shift(ndp, 1))
        b = lax.ppermute(b, "dp", _shift(ndp, -1))
        pieces.append(((j - s) % ndp, 0, a))
        pieces.append(((j + s) % ndp, 1, b))

    gu_pre = None
    grad_hidden = None
    weights_full = jnp.zeros((rows * ndp, 2 * ff), jnp.bfloat16)
    for src, h, piece in pieces:
        start = src * rows + h * half
        xs = lax.dynamic_slice_in_dim(inputs, start, half, axis=1)
        gs = lax.dynamic_slice_in_dim(upstream, start, half, axis=1)
        p1 = jnp.dot(xs, piece[:, : 2 * ff], preferred_element_type=jnp.float32)
        p2 = jnp.dot(gs, piece[:, 2 * ff :], preferred_element_type=jnp.float32)
        gu_pre = p1 if gu_pre is None else gu_pre + p1
        grad_hidden = p2 if grad_hidden is None else grad_hidden + p2
        weights_full = lax.dynamic_update_slice(weights_full, piece[:, : 2 * ff], (start, 0))

    gate_pre = gu_pre[:, :ff]
    up_pre = gu_pre[:, ff:]
    gate_sigmoid = jax.nn.sigmoid(gate_pre)
    active = gate_pre * gate_sigmoid
    hidden = (active * up_pre).astype(jnp.bfloat16)
    grad_up = (grad_hidden * active).astype(jnp.bfloat16)
    grad_gate = (
        grad_hidden * up_pre * gate_sigmoid * (1.0 + gate_pre * (1.0 - gate_sigmoid))
    ).astype(jnp.bfloat16)

    full_grad = lax.dot_general(
        hidden, upstream, (((0,), (0,)), ((), ())), preferred_element_type=jnp.float32
    )
    cols = full_grad.shape[1] // ndp
    grad_down = lax.dynamic_slice_in_dim(full_grad, j * cols, cols, axis=1)
    for s in range(1, ndp):
        blk = lax.dynamic_slice_in_dim(full_grad, ((j + s) % ndp) * cols, cols, axis=1)
        got = lax.ppermute(blk.astype(jnp.bfloat16), "dp", _shift(ndp, s))
        grad_down = grad_down + got.astype(jnp.float32)

    both = jnp.concatenate([grad_gate, grad_up], axis=1)
    partial_sum = lax.dot_general(
        both, weights_full, (((1,), (1,)), ((), ())), preferred_element_type=jnp.float32
    )
    input_grad = lax.psum_scatter(
        partial_sum.astype(jnp.bfloat16), "mp", scatter_dimension=0, tiled=True
    )

    first_new = 0.9 * first_moment[0] + 0.1 * grad_down
    second_new = 0.999 * second_moment[0] + 0.001 * grad_down * grad_down
    adam_step = first_new / bias_one / (jnp.sqrt(second_new / bias_two) + 1e-08) + 0.1 * master
    inner_params = master - 0.001 * adam_step
    drift_local = anchor - inner_params

    nout = lax.axis_size("outer")
    total = drift_local.astype(jnp.bfloat16)
    step = 1
    while step < nout:
        perm = [(i, i ^ step) for i in range(nout)]
        mine = total.astype(jnp.bfloat16)
        total = mine.astype(jnp.float32) + lax.ppermute(mine, "outer", perm).astype(jnp.float32)
        step *= 2
    mean_drift = total / nout
    momentum_out = 0.9 * outer_momentum + mean_drift
    new_params = anchor - 0.7 * (mean_drift + 0.9 * momentum_out)
    return (new_params, first_new[None], second_new[None], momentum_out, input_grad[None])


def solution(mesh):
    return jax.shard_map(
        shards,
        mesh=mesh,
        in_specs=(
            P("outer", "dp", None),
            P("outer", "dp", None),
            P("outer", "dp", "mp"),
            P("outer", "dp", "mp"),
            P("outer", "mp", "dp"),
            P("outer", "mp", "dp"),
            P("outer", "mp", "dp"),
            P("mp", "dp"),
            P("mp", "dp"),
        ),
        out_specs=(
            P("mp", "dp"),
            P("outer", "mp", "dp"),
            P("outer", "mp", "dp"),
            P("mp", "dp"),
            P("outer", ("dp", "mp"), None),
        ),
        check_vma=False,
    )
```

```python
import jax
import jax.numpy as jnp
from jax import lax
from jax.sharding import PartitionSpec as P

bias_one = 1.0 - (0.9**50) ** 2
bias_two = 1.0 - (0.999**50) ** 2


def _shift(n, s):
    return [(i, (i + s) % n) for i in range(n)]


def _ring_reduce_scatter(part):
    nmp = lax.axis_size("mp")
    m = lax.axis_index("mp")
    nlo = 2
    nz = nmp // nlo
    z = m // nlo
    lo = m % nlo
    rows = part.shape[0] // nz
    halfc = part.shape[1] // 2
    up = [(i, ((i // nlo + 1) % nz) * nlo + i % nlo) for i in range(nmp)]
    down = [(i, ((i // nlo - 1) % nz) * nlo + i % nlo) for i in range(nmp)]

    def chunk(c, h):
        blk = lax.dynamic_slice_in_dim(part, c * rows, rows, axis=0)
        return blk[:, h * halfc : (h + 1) * halfc].astype(jnp.float32)

    acc_a = chunk((z - 1) % nz, 0)
    acc_b = chunk((z + 1) % nz, 1)
    for t in range(1, nz):
        got_a = lax.ppermute(acc_a.astype(jnp.bfloat16), "mp", up)
        got_b = lax.ppermute(acc_b.astype(jnp.bfloat16), "mp", down)
        acc_a = got_a.astype(jnp.float32) + chunk((z - t - 1) % nz, 0)
        acc_b = got_b.astype(jnp.float32) + chunk((z + t + 1) % nz, 1)
    acc = jnp.concatenate([acc_a, acc_b], axis=1)
    sub = rows // nlo
    mine = lax.dynamic_slice_in_dim(acc, lo * sub, sub, axis=0)
    other = lax.dynamic_slice_in_dim(acc, (1 - lo) * sub, sub, axis=0)
    got = lax.ppermute(other.astype(jnp.bfloat16), "mp", [(i, i ^ 1) for i in range(nmp)])
    return (mine + got.astype(jnp.float32)).astype(jnp.bfloat16)


def shards(
    tokens,
    cotangent,
    gate_weight,
    up_weight,
    down_master,
    first_moment,
    second_moment,
    anchor,
    outer_momentum,
):
    ndp = lax.axis_size("dp")
    j = lax.axis_index("dp")
    inputs = tokens[0]
    upstream = cotangent[0]
    master = down_master[0]
    down_half = master.astype(jnp.bfloat16)
    ff = master.shape[0]

    shard = jnp.concatenate([gate_weight[0], up_weight[0], down_half.T], axis=1)
    rows = shard.shape[0]
    half = rows // 2
    a, b = shard[:half], shard[half:]
    pieces = [(j, 0, a), (j, 1, b)]
    for s in range(1, ndp):
        a = lax.ppermute(a, "dp", _shift(ndp, 1))
        b = lax.ppermute(b, "dp", _shift(ndp, -1))
        pieces.append(((j - s) % ndp, 0, a))
        pieces.append(((j + s) % ndp, 1, b))

    gu_pre = None
    grad_hidden = None
    weights_full = jnp.zeros((rows * ndp, 2 * ff), jnp.bfloat16)
    for src, h, piece in pieces:
        start = src * rows + h * half
        xs = lax.dynamic_slice_in_dim(inputs, start, half, axis=1)
        gs = lax.dynamic_slice_in_dim(upstream, start, half, axis=1)
        p1 = jnp.dot(xs, piece[:, : 2 * ff], preferred_element_type=jnp.float32)
        p2 = jnp.dot(gs, piece[:, 2 * ff :], preferred_element_type=jnp.float32)
        gu_pre = p1 if gu_pre is None else gu_pre + p1
        grad_hidden = p2 if grad_hidden is None else grad_hidden + p2
        weights_full = lax.dynamic_update_slice(weights_full, piece[:, : 2 * ff], (start, 0))

    gate_pre = gu_pre[:, :ff]
    up_pre = gu_pre[:, ff:]
    gate_sigmoid = jax.nn.sigmoid(gate_pre)
    active = gate_pre * gate_sigmoid
    hidden = (active * up_pre).astype(jnp.bfloat16)
    grad_up = (grad_hidden * active).astype(jnp.bfloat16)
    grad_gate = (
        grad_hidden * up_pre * gate_sigmoid * (1.0 + gate_pre * (1.0 - gate_sigmoid))
    ).astype(jnp.bfloat16)

    full_grad = lax.dot_general(
        hidden, upstream, (((0,), (0,)), ((), ())), preferred_element_type=jnp.float32
    )
    cols = full_grad.shape[1] // ndp
    grad_down = lax.dynamic_slice_in_dim(full_grad, j * cols, cols, axis=1)
    for s in range(1, ndp):
        blk = lax.dynamic_slice_in_dim(full_grad, ((j + s) % ndp) * cols, cols, axis=1)
        got = lax.ppermute(blk.astype(jnp.bfloat16), "dp", _shift(ndp, s))
        grad_down = grad_down + got.astype(jnp.float32)

    both = jnp.concatenate([grad_gate, grad_up], axis=1)
    partial_sum = lax.dot_general(
        both, weights_full, (((1,), (1,)), ((), ())), preferred_element_type=jnp.float32
    )
    input_grad = _ring_reduce_scatter(partial_sum.astype(jnp.bfloat16))

    first_new = 0.9 * first_moment[0] + 0.1 * grad_down
    second_new = 0.999 * second_moment[0] + 0.001 * grad_down * grad_down
    adam_step = first_new / bias_one / (jnp.sqrt(second_new / bias_two) + 1e-08) + 0.1 * master
    inner_params = master - 0.001 * adam_step
    drift_local = anchor - inner_params

    nout = lax.axis_size("outer")
    total = drift_local.astype(jnp.bfloat16)
    step = 1
    while step < nout:
        perm = [(i, i ^ step) for i in range(nout)]
        mine = total.astype(jnp.bfloat16)
        total = mine.astype(jnp.float32) + lax.ppermute(mine, "outer", perm).astype(jnp.float32)
        step *= 2
    mean_drift = total / nout
    momentum_out = 0.9 * outer_momentum + mean_drift
    new_params = anchor - 0.7 * (mean_drift + 0.9 * momentum_out)
    return (new_params, first_new[None], second_new[None], momentum_out, input_grad[None])


def solution(mesh):
    return jax.shard_map(
        shards,
        mesh=mesh,
        in_specs=(
            P("outer", "dp", None),
            P("outer", "dp", None),
            P("outer", "dp", "mp"),
            P("outer", "dp", "mp"),
            P("outer", "mp", "dp"),
            P("outer", "mp", "dp"),
            P("outer", "mp", "dp"),
            P("mp", "dp"),
            P("mp", "dp"),
        ),
        out_specs=(
            P("mp", "dp"),
            P("outer", "mp", "dp"),
            P("outer", "mp", "dp"),
            P("mp", "dp"),
            P("outer", ("dp", "mp"), None),
        ),
        check_vma=False,
    )
```

```python
import jax
import jax.numpy as jnp
from jax import lax
from jax.sharding import PartitionSpec as P

bias_one = 1.0 - (0.9**50) ** 2
bias_two = 1.0 - (0.999**50) ** 2


def _shift(n, s):
    return [(i, (i + s) % n) for i in range(n)]


def _ring_reduce_scatter(part):
    nmp = lax.axis_size("mp")
    m = lax.axis_index("mp")
    nlo = 2
    nz = nmp // nlo
    far = nz // 2
    z = m // nlo
    lo = m % nlo
    rows = part.shape[0] // nz
    halfc = part.shape[1] // 2
    up = [(i, ((i // nlo + 1) % nz) * nlo + i % nlo) for i in range(nmp)]
    down = [(i, ((i // nlo - 1) % nz) * nlo + i % nlo) for i in range(nmp)]

    def chunk(c):
        return lax.dynamic_slice_in_dim(part, (c % nz) * rows, rows, axis=0).astype(jnp.float32)

    first = chunk(z + far)
    send_a = first[:, :halfc]
    send_b = first[:, halfc:]
    for r in range(2, far + 2):
        got_a = lax.ppermute(send_a.astype(jnp.bfloat16), "mp", up).astype(jnp.float32)
        got_b = lax.ppermute(send_b.astype(jnp.bfloat16), "mp", down).astype(jnp.float32)
        own_a = chunk(z + far + 1 - r)
        own_b = chunk(z - far - 1 + r)
        if r == 2:
            got_a = jnp.concatenate([got_a, jnp.zeros_like(got_a)], axis=1)
            got_b = jnp.concatenate([jnp.zeros_like(got_b), got_b], axis=1)
        if r <= far:
            send_a = got_a + own_a
            send_b = got_b + own_b
    acc = own_a + got_a + got_b
    sub = rows // nlo
    mine = lax.dynamic_slice_in_dim(acc, lo * sub, sub, axis=0)
    other = lax.dynamic_slice_in_dim(acc, (1 - lo) * sub, sub, axis=0)
    got = lax.ppermute(other.astype(jnp.bfloat16), "mp", [(i, i ^ 1) for i in range(nmp)])
    return (mine + got.astype(jnp.float32)).astype(jnp.bfloat16)


def shards(
    tokens,
    cotangent,
    gate_weight,
    up_weight,
    down_master,
    first_moment,
    second_moment,
    anchor,
    outer_momentum,
):
    ndp = lax.axis_size("dp")
    j = lax.axis_index("dp")
    inputs = tokens[0]
    upstream = cotangent[0]
    master = down_master[0]
    down_half = master.astype(jnp.bfloat16)
    ff = master.shape[0]

    assert ndp == 4
    shard = jnp.concatenate([gate_weight[0], up_weight[0], down_half.T], axis=1)
    rows = shard.shape[0]
    half = rows // 2
    from_left = lax.ppermute(shard, "dp", _shift(ndp, 1))
    from_right = lax.ppermute(shard, "dp", _shift(ndp, -1))
    far_a = lax.ppermute(from_left[:half], "dp", _shift(ndp, 1))
    far_b = lax.ppermute(from_right[half:], "dp", _shift(ndp, -1))
    pieces = [
        (j * rows, shard),
        (((j - 1) % ndp) * rows, from_left),
        (((j + 1) % ndp) * rows, from_right),
        (((j + 2) % ndp) * rows, far_a),
        (((j + 2) % ndp) * rows + half, far_b),
    ]

    gu_pre = None
    grad_hidden = None
    weights_full = jnp.zeros((rows * ndp, 2 * ff), jnp.bfloat16)
    for start, piece in pieces:
        size = piece.shape[0]
        xs = lax.dynamic_slice_in_dim(inputs, start, size, axis=1)
        gs = lax.dynamic_slice_in_dim(upstream, start, size, axis=1)
        p1 = jnp.dot(xs, piece[:, : 2 * ff], preferred_element_type=jnp.float32)
        p2 = jnp.dot(gs, piece[:, 2 * ff :], preferred_element_type=jnp.float32)
        gu_pre = p1 if gu_pre is None else gu_pre + p1
        grad_hidden = p2 if grad_hidden is None else grad_hidden + p2
        weights_full = lax.dynamic_update_slice(weights_full, piece[:, : 2 * ff], (start, 0))

    gate_pre = gu_pre[:, :ff]
    up_pre = gu_pre[:, ff:]
    gate_sigmoid = jax.nn.sigmoid(gate_pre)
    active = gate_pre * gate_sigmoid
    hidden = (active * up_pre).astype(jnp.bfloat16)
    grad_up = (grad_hidden * active).astype(jnp.bfloat16)
    grad_gate = (
        grad_hidden * up_pre * gate_sigmoid * (1.0 + gate_pre * (1.0 - gate_sigmoid))
    ).astype(jnp.bfloat16)

    full_grad = lax.dot_general(
        hidden, upstream, (((0,), (0,)), ((), ())), preferred_element_type=jnp.float32
    )
    cols = full_grad.shape[1] // ndp
    grad_down = lax.dynamic_slice_in_dim(full_grad, j * cols, cols, axis=1)
    for s in range(1, ndp):
        blk = lax.dynamic_slice_in_dim(full_grad, ((j + s) % ndp) * cols, cols, axis=1)
        got = lax.ppermute(blk.astype(jnp.bfloat16), "dp", _shift(ndp, s))
        grad_down = grad_down + got.astype(jnp.float32)

    both = jnp.concatenate([grad_gate, grad_up], axis=1)
    partial_sum = lax.dot_general(
        both, weights_full, (((1,), (1,)), ((), ())), preferred_element_type=jnp.float32
    )
    input_grad = _ring_reduce_scatter(partial_sum.astype(jnp.bfloat16))

    first_new = 0.9 * first_moment[0] + 0.1 * grad_down
    second_new = 0.999 * second_moment[0] + 0.001 * grad_down * grad_down
    adam_step = first_new / bias_one / (jnp.sqrt(second_new / bias_two) + 1e-08) + 0.1 * master
    inner_params = master - 0.001 * adam_step
    drift_local = anchor - inner_params

    nout = lax.axis_size("outer")
    total = drift_local.astype(jnp.bfloat16)
    step = 1
    while step < nout:
        perm = [(i, i ^ step) for i in range(nout)]
        mine = total.astype(jnp.bfloat16)
        total = mine.astype(jnp.float32) + lax.ppermute(mine, "outer", perm).astype(jnp.float32)
        step *= 2
    mean_drift = total / nout
    momentum_out = 0.9 * outer_momentum + mean_drift
    new_params = anchor - 0.7 * (mean_drift + 0.9 * momentum_out)
    return (new_params, first_new[None], second_new[None], momentum_out, input_grad[None])


def solution(mesh):
    return jax.shard_map(
        shards,
        mesh=mesh,
        in_specs=(
            P("outer", "dp", None),
            P("outer", "dp", None),
            P("outer", "dp", "mp"),
            P("outer", "dp", "mp"),
            P("outer", "mp", "dp"),
            P("outer", "mp", "dp"),
            P("outer", "mp", "dp"),
            P("mp", "dp"),
            P("mp", "dp"),
        ),
        out_specs=(
            P("mp", "dp"),
            P("outer", "mp", "dp"),
            P("outer", "mp", "dp"),
            P("mp", "dp"),
            P("outer", ("dp", "mp"), None),
        ),
        check_vma=False,
    )
```

```python
import jax
import jax.numpy as jnp
from jax import lax
from jax.sharding import PartitionSpec as P

bias_one = 1.0 - (0.9**50) ** 2
bias_two = 1.0 - (0.999**50) ** 2


def _shift(n, s):
    return [(i, (i + s) % n) for i in range(n)]


def _z_reduce_scatter(chunks, z, nz, up, down):
    far = nz // 2
    halfc = chunks.shape[2] // 2

    def chunk(c):
        return lax.dynamic_index_in_dim(chunks, c % nz, axis=0, keepdims=False).astype(jnp.float32)

    first = chunk(z + far)
    send_a = first[:, :halfc]
    send_b = first[:, halfc:]
    for r in range(2, far + 2):
        got_a = lax.ppermute(send_a.astype(jnp.bfloat16), "mp", up).astype(jnp.float32)
        got_b = lax.ppermute(send_b.astype(jnp.bfloat16), "mp", down).astype(jnp.float32)
        own_a = chunk(z + far + 1 - r)
        own_b = chunk(z - far - 1 + r)
        if r == 2:
            got_a = jnp.concatenate([got_a, jnp.zeros_like(got_a)], axis=1)
            got_b = jnp.concatenate([jnp.zeros_like(got_b), got_b], axis=1)
        if r <= far:
            send_a = got_a + own_a
            send_b = got_b + own_b
    return own_a + got_a + got_b


def _ring_reduce_scatter(part):
    nmp = lax.axis_size("mp")
    m = lax.axis_index("mp")
    nlo = 2
    nz = nmp // nlo
    z = m // nlo
    lo = m % nlo
    rows = part.shape[0] // nz
    sub = rows // nlo
    halfc = part.shape[1] // 2
    up = [(i, ((i // nlo + 1) % nz) * nlo + i % nlo) for i in range(nmp)]
    down = [(i, ((i // nlo - 1) % nz) * nlo + i % nlo) for i in range(nmp)]
    pair = [(i, i ^ 1) for i in range(nmp)]

    py = part[:, halfc:].reshape(nz, nlo, sub, halfc)
    keep = lax.dynamic_index_in_dim(py, lo, axis=1, keepdims=False)
    give = lax.dynamic_index_in_dim(py, 1 - lo, axis=1, keepdims=False)
    got_y = lax.ppermute(give, "mp", pair)
    acc_y = keep.astype(jnp.float32) + got_y.astype(jnp.float32)

    pz = part[:, :halfc].reshape(nz, rows, halfc)
    acc_z = _z_reduce_scatter(pz, z, nz, up, down)
    mine = lax.dynamic_slice_in_dim(acc_z, lo * sub, sub, axis=0)
    other = lax.dynamic_slice_in_dim(acc_z, (1 - lo) * sub, sub, axis=0)
    got = lax.ppermute(other.astype(jnp.bfloat16), "mp", pair)
    out_z = mine + got.astype(jnp.float32)

    out_y = _z_reduce_scatter(acc_y.astype(jnp.bfloat16), z, nz, up, down)
    return jnp.concatenate([out_z, out_y], axis=1).astype(jnp.bfloat16)


def shards(
    tokens,
    cotangent,
    gate_weight,
    up_weight,
    down_master,
    first_moment,
    second_moment,
    anchor,
    outer_momentum,
):
    ndp = lax.axis_size("dp")
    j = lax.axis_index("dp")
    inputs = tokens[0]
    upstream = cotangent[0]
    master = down_master[0]
    down_half = master.astype(jnp.bfloat16)
    ff = master.shape[0]

    assert ndp == 4
    shard = jnp.concatenate([gate_weight[0], up_weight[0], down_half.T], axis=1)
    rows = shard.shape[0]
    half = rows // 2
    from_left = lax.ppermute(shard, "dp", _shift(ndp, 1))
    from_right = lax.ppermute(shard, "dp", _shift(ndp, -1))
    far_a = lax.ppermute(from_left[:half], "dp", _shift(ndp, 1))
    far_b = lax.ppermute(from_right[half:], "dp", _shift(ndp, -1))
    pieces = [
        (j * rows, shard),
        (((j - 1) % ndp) * rows, from_left),
        (((j + 1) % ndp) * rows, from_right),
        (((j + 2) % ndp) * rows, far_a),
        (((j + 2) % ndp) * rows + half, far_b),
    ]

    gu_pre = None
    grad_hidden = None
    weights_full = jnp.zeros((rows * ndp, 2 * ff), jnp.bfloat16)
    for start, piece in pieces:
        size = piece.shape[0]
        xs = lax.dynamic_slice_in_dim(inputs, start, size, axis=1)
        gs = lax.dynamic_slice_in_dim(upstream, start, size, axis=1)
        p1 = jnp.dot(xs, piece[:, : 2 * ff], preferred_element_type=jnp.float32)
        p2 = jnp.dot(gs, piece[:, 2 * ff :], preferred_element_type=jnp.float32)
        gu_pre = p1 if gu_pre is None else gu_pre + p1
        grad_hidden = p2 if grad_hidden is None else grad_hidden + p2
        weights_full = lax.dynamic_update_slice(weights_full, piece[:, : 2 * ff], (start, 0))

    gate_pre = gu_pre[:, :ff]
    up_pre = gu_pre[:, ff:]
    gate_sigmoid = jax.nn.sigmoid(gate_pre)
    active = gate_pre * gate_sigmoid
    hidden = (active * up_pre).astype(jnp.bfloat16)
    grad_up = (grad_hidden * active).astype(jnp.bfloat16)
    grad_gate = (
        grad_hidden * up_pre * gate_sigmoid * (1.0 + gate_pre * (1.0 - gate_sigmoid))
    ).astype(jnp.bfloat16)

    full_grad = lax.dot_general(
        hidden, upstream, (((0,), (0,)), ((), ())), preferred_element_type=jnp.float32
    )
    cols = full_grad.shape[1] // ndp
    grad_down = lax.dynamic_slice_in_dim(full_grad, j * cols, cols, axis=1)
    for s in range(1, ndp):
        blk = lax.dynamic_slice_in_dim(full_grad, ((j + s) % ndp) * cols, cols, axis=1)
        got = lax.ppermute(blk.astype(jnp.bfloat16), "dp", _shift(ndp, s))
        grad_down = grad_down + got.astype(jnp.float32)

    both = jnp.concatenate([grad_gate, grad_up], axis=1)
    partial_sum = lax.dot_general(
        both, weights_full, (((1,), (1,)), ((), ())), preferred_element_type=jnp.float32
    )
    input_grad = _ring_reduce_scatter(partial_sum.astype(jnp.bfloat16))

    first_new = 0.9 * first_moment[0] + 0.1 * grad_down
    second_new = 0.999 * second_moment[0] + 0.001 * grad_down * grad_down
    adam_step = first_new / bias_one / (jnp.sqrt(second_new / bias_two) + 1e-08) + 0.1 * master
    inner_params = master - 0.001 * adam_step
    drift_local = anchor - inner_params

    nout = lax.axis_size("outer")
    total = drift_local.astype(jnp.bfloat16)
    step = 1
    while step < nout:
        perm = [(i, i ^ step) for i in range(nout)]
        mine = total.astype(jnp.bfloat16)
        total = mine.astype(jnp.float32) + lax.ppermute(mine, "outer", perm).astype(jnp.float32)
        step *= 2
    mean_drift = total / nout
    momentum_out = 0.9 * outer_momentum + mean_drift
    new_params = anchor - 0.7 * (mean_drift + 0.9 * momentum_out)
    return (new_params, first_new[None], second_new[None], momentum_out, input_grad[None])


def solution(mesh):
    return jax.shard_map(
        shards,
        mesh=mesh,
        in_specs=(
            P("outer", "dp", None),
            P("outer", "dp", None),
            P("outer", "dp", "mp"),
            P("outer", "dp", "mp"),
            P("outer", "mp", "dp"),
            P("outer", "mp", "dp"),
            P("outer", "mp", "dp"),
            P("mp", "dp"),
            P("mp", "dp"),
        ),
        out_specs=(
            P("mp", "dp"),
            P("outer", "mp", "dp"),
            P("outer", "mp", "dp"),
            P("mp", "dp"),
            P("outer", ("dp", "mp"), None),
        ),
        check_vma=False,
    )
```

```python
import jax
import jax.numpy as jnp
from jax import lax
from jax.sharding import PartitionSpec as P

bias_one = 1.0 - (0.9**50) ** 2
bias_two = 1.0 - (0.999**50) ** 2


def _shift(n, s):
    return [(i, (i + s) % n) for i in range(n)]


def _z_reduce_scatter(chunks, z, nz, up, down):
    far = nz // 2
    halfc = chunks.shape[2] // 2

    def chunk(c):
        return lax.dynamic_index_in_dim(chunks, c % nz, axis=0, keepdims=False).astype(jnp.float32)

    first = chunk(z + far)
    send_a = first[:, :halfc]
    send_b = first[:, halfc:]
    for r in range(2, far + 2):
        got_a = lax.ppermute(send_a.astype(jnp.bfloat16), "mp", up).astype(jnp.float32)
        got_b = lax.ppermute(send_b.astype(jnp.bfloat16), "mp", down).astype(jnp.float32)
        own_a = chunk(z + far + 1 - r)
        own_b = chunk(z - far - 1 + r)
        if r == 2:
            got_a = jnp.concatenate([got_a, jnp.zeros_like(got_a)], axis=1)
            got_b = jnp.concatenate([jnp.zeros_like(got_b), got_b], axis=1)
        if r <= far:
            send_a = got_a + own_a
            send_b = got_b + own_b
    return own_a + got_a + got_b


def _ring_reduce_scatter(part_z, part_y):
    nmp = lax.axis_size("mp")
    m = lax.axis_index("mp")
    nlo = 2
    nz = nmp // nlo
    z = m // nlo
    lo = m % nlo
    rows = part_z.shape[0] // nz
    sub = rows // nlo
    halfc = part_z.shape[1]
    up = [(i, ((i // nlo + 1) % nz) * nlo + i % nlo) for i in range(nmp)]
    down = [(i, ((i // nlo - 1) % nz) * nlo + i % nlo) for i in range(nmp)]
    pair = [(i, i ^ 1) for i in range(nmp)]

    out_y = lax.psum_scatter(part_y, "mp", scatter_dimension=0, tiled=True)

    pz = part_z.reshape(nz, rows, halfc)
    acc_z = _z_reduce_scatter(pz, z, nz, up, down)
    mine = lax.dynamic_slice_in_dim(acc_z, lo * sub, sub, axis=0)
    other = lax.dynamic_slice_in_dim(acc_z, (1 - lo) * sub, sub, axis=0)
    got = lax.ppermute(other.astype(jnp.bfloat16), "mp", pair)
    out_z = mine + got.astype(jnp.float32)

    return jnp.concatenate([out_z.astype(jnp.bfloat16), out_y], axis=1)


def shards(
    tokens,
    cotangent,
    gate_weight,
    up_weight,
    down_master,
    first_moment,
    second_moment,
    anchor,
    outer_momentum,
):
    ndp = lax.axis_size("dp")
    j = lax.axis_index("dp")
    inputs = tokens[0]
    upstream = cotangent[0]
    master = down_master[0]
    down_half = master.astype(jnp.bfloat16)
    ff = master.shape[0]

    assert ndp == 4
    shard = jnp.concatenate([gate_weight[0], up_weight[0], down_half.T], axis=1)
    rows = shard.shape[0]
    half = rows // 2
    from_left = lax.ppermute(shard, "dp", _shift(ndp, 1))
    from_right = lax.ppermute(shard, "dp", _shift(ndp, -1))
    far_a = lax.ppermute(from_left[:half], "dp", _shift(ndp, 1))
    far_b = lax.ppermute(from_right[half:], "dp", _shift(ndp, -1))
    pieces = [
        (j * rows, shard),
        (((j - 1) % ndp) * rows, from_left),
        (((j + 1) % ndp) * rows, from_right),
        (((j + 2) % ndp) * rows, far_a),
        (((j + 2) % ndp) * rows + half, far_b),
    ]

    gu_pre = None
    grad_hidden = None
    weights_full = jnp.zeros((rows * ndp, 2 * ff), jnp.bfloat16)
    for start, piece in pieces:
        size = piece.shape[0]
        xs = lax.dynamic_slice_in_dim(inputs, start, size, axis=1)
        gs = lax.dynamic_slice_in_dim(upstream, start, size, axis=1)
        p1 = jnp.dot(xs, piece[:, : 2 * ff], preferred_element_type=jnp.float32)
        p2 = jnp.dot(gs, piece[:, 2 * ff :], preferred_element_type=jnp.float32)
        gu_pre = p1 if gu_pre is None else gu_pre + p1
        grad_hidden = p2 if grad_hidden is None else grad_hidden + p2
        weights_full = lax.dynamic_update_slice(weights_full, piece[:, : 2 * ff], (start, 0))

    gate_pre = gu_pre[:, :ff]
    up_pre = gu_pre[:, ff:]
    gate_sigmoid = jax.nn.sigmoid(gate_pre)
    active = gate_pre * gate_sigmoid
    hidden = (active * up_pre).astype(jnp.bfloat16)
    grad_up = (grad_hidden * active).astype(jnp.bfloat16)
    grad_gate = (
        grad_hidden * up_pre * gate_sigmoid * (1.0 + gate_pre * (1.0 - gate_sigmoid))
    ).astype(jnp.bfloat16)

    full_grad = lax.dot_general(
        hidden, upstream, (((0,), (0,)), ((), ())), preferred_element_type=jnp.float32
    )
    cols = full_grad.shape[1] // ndp
    grad_down = lax.dynamic_slice_in_dim(full_grad, j * cols, cols, axis=1)
    for s in range(1, ndp):
        blk = lax.dynamic_slice_in_dim(full_grad, ((j + s) % ndp) * cols, cols, axis=1)
        got = lax.ppermute(blk.astype(jnp.bfloat16), "dp", _shift(ndp, s))
        grad_down = grad_down + got.astype(jnp.float32)

    both = jnp.concatenate([grad_gate, grad_up], axis=1)
    dcols = weights_full.shape[0] // 2
    part_y = lax.dot_general(
        both, weights_full[dcols:], (((1,), (1,)), ((), ())), preferred_element_type=jnp.float32
    ).astype(jnp.bfloat16)
    part_y, both = lax.optimization_barrier((part_y, both))
    part_z = lax.dot_general(
        both, weights_full[:dcols], (((1,), (1,)), ((), ())), preferred_element_type=jnp.float32
    ).astype(jnp.bfloat16)
    input_grad = _ring_reduce_scatter(part_z, part_y)

    first_new = 0.9 * first_moment[0] + 0.1 * grad_down
    second_new = 0.999 * second_moment[0] + 0.001 * grad_down * grad_down
    adam_step = first_new / bias_one / (jnp.sqrt(second_new / bias_two) + 1e-08) + 0.1 * master
    inner_params = master - 0.001 * adam_step
    drift_local = anchor - inner_params

    nout = lax.axis_size("outer")
    total = drift_local.astype(jnp.bfloat16)
    step = 1
    while step < nout:
        perm = [(i, i ^ step) for i in range(nout)]
        mine = total.astype(jnp.bfloat16)
        total = mine.astype(jnp.float32) + lax.ppermute(mine, "outer", perm).astype(jnp.float32)
        step *= 2
    mean_drift = total / nout
    momentum_out = 0.9 * outer_momentum + mean_drift
    new_params = anchor - 0.7 * (mean_drift + 0.9 * momentum_out)
    return (new_params, first_new[None], second_new[None], momentum_out, input_grad[None])


def solution(mesh):
    return jax.shard_map(
        shards,
        mesh=mesh,
        in_specs=(
            P("outer", "dp", None),
            P("outer", "dp", None),
            P("outer", "dp", "mp"),
            P("outer", "dp", "mp"),
            P("outer", "mp", "dp"),
            P("outer", "mp", "dp"),
            P("outer", "mp", "dp"),
            P("mp", "dp"),
            P("mp", "dp"),
        ),
        out_specs=(
            P("mp", "dp"),
            P("outer", "mp", "dp"),
            P("outer", "mp", "dp"),
            P("mp", "dp"),
            P("outer", ("dp", "mp"), None),
        ),
        check_vma=False,
    )
```

```python
import jax
import jax.numpy as jnp
from jax import lax
from jax.sharding import PartitionSpec as P

bias_one = 1.0 - (0.9**50) ** 2
bias_two = 1.0 - (0.999**50) ** 2


def _shift(n, s):
    return [(i, (i + s) % n) for i in range(n)]


def _z_reduce_scatter(chunks, z, nz, up, down, sync=None, sync_round=3):
    far = nz // 2
    halfc = chunks.shape[2] // 2

    def chunk(c):
        return lax.dynamic_index_in_dim(chunks, c % nz, axis=0, keepdims=False).astype(jnp.float32)

    first = chunk(z + far)
    send_a = first[:, :halfc]
    send_b = first[:, halfc:]
    for r in range(2, far + 2):
        if sync is not None and r == sync_round + 1:
            send_a, send_b, sync = lax.optimization_barrier((send_a, send_b, sync))
        got_a = lax.ppermute(send_a.astype(jnp.bfloat16), "mp", up).astype(jnp.float32)
        got_b = lax.ppermute(send_b.astype(jnp.bfloat16), "mp", down).astype(jnp.float32)
        own_a = chunk(z + far + 1 - r)
        own_b = chunk(z - far - 1 + r)
        if r == 2:
            got_a = jnp.concatenate([got_a, jnp.zeros_like(got_a)], axis=1)
            got_b = jnp.concatenate([jnp.zeros_like(got_b), got_b], axis=1)
        if r <= far:
            send_a = got_a + own_a
            send_b = got_b + own_b
    out = own_a + got_a + got_b
    return out if sync is None else (out, sync)


def _ring_reduce_scatter(part_z, part_y):
    nmp = lax.axis_size("mp")
    m = lax.axis_index("mp")
    nlo = 2
    nz = nmp // nlo
    z = m // nlo
    lo = m % nlo
    rows = part_z.shape[0] // nz
    sub = rows // nlo
    halfc = part_z.shape[1]
    up = [(i, ((i // nlo + 1) % nz) * nlo + i % nlo) for i in range(nmp)]
    down = [(i, ((i // nlo - 1) % nz) * nlo + i % nlo) for i in range(nmp)]
    pair = [(i, i ^ 1) for i in range(nmp)]

    py = part_y.reshape(nz, nlo, sub, halfc)
    keep = lax.dynamic_index_in_dim(py, lo, axis=1, keepdims=False)
    give = lax.dynamic_index_in_dim(py, 1 - lo, axis=1, keepdims=False)
    got_y = lax.ppermute(give, "mp", pair)

    pz = part_z.reshape(nz, rows, halfc)
    acc_z, got_y = _z_reduce_scatter(pz, z, nz, up, down, sync=got_y)
    acc_y = keep.astype(jnp.float32) + got_y.astype(jnp.float32)
    mine = lax.dynamic_slice_in_dim(acc_z, lo * sub, sub, axis=0)
    other = lax.dynamic_slice_in_dim(acc_z, (1 - lo) * sub, sub, axis=0)
    got = lax.ppermute(other.astype(jnp.bfloat16), "mp", pair)
    out_z = mine + got.astype(jnp.float32)

    out_y = _z_reduce_scatter(acc_y.astype(jnp.bfloat16), z, nz, up, down)
    return jnp.concatenate([out_z, out_y], axis=1).astype(jnp.bfloat16)


def shards(
    tokens,
    cotangent,
    gate_weight,
    up_weight,
    down_master,
    first_moment,
    second_moment,
    anchor,
    outer_momentum,
):
    ndp = lax.axis_size("dp")
    j = lax.axis_index("dp")
    inputs = tokens[0]
    upstream = cotangent[0]
    master = down_master[0]
    down_half = master.astype(jnp.bfloat16)
    ff = master.shape[0]

    assert ndp == 4
    shard = jnp.concatenate([gate_weight[0], up_weight[0], down_half.T], axis=1)
    rows = shard.shape[0]
    half = rows // 2
    from_left = lax.ppermute(shard, "dp", _shift(ndp, 1))
    from_right = lax.ppermute(shard, "dp", _shift(ndp, -1))
    far_a = lax.ppermute(from_left[:half], "dp", _shift(ndp, 1))
    far_b = lax.ppermute(from_right[half:], "dp", _shift(ndp, -1))
    pieces = [
        (j * rows, shard),
        (((j - 1) % ndp) * rows, from_left),
        (((j + 1) % ndp) * rows, from_right),
        (((j + 2) % ndp) * rows, far_a),
        (((j + 2) % ndp) * rows + half, far_b),
    ]

    gu_pre = None
    grad_hidden = None
    weights_full = jnp.zeros((rows * ndp, 2 * ff), jnp.bfloat16)
    for start, piece in pieces:
        size = piece.shape[0]
        xs = lax.dynamic_slice_in_dim(inputs, start, size, axis=1)
        gs = lax.dynamic_slice_in_dim(upstream, start, size, axis=1)
        p1 = jnp.dot(xs, piece[:, : 2 * ff], preferred_element_type=jnp.float32)
        p2 = jnp.dot(gs, piece[:, 2 * ff :], preferred_element_type=jnp.float32)
        gu_pre = p1 if gu_pre is None else gu_pre + p1
        grad_hidden = p2 if grad_hidden is None else grad_hidden + p2
        weights_full = lax.dynamic_update_slice(weights_full, piece[:, : 2 * ff], (start, 0))

    gate_pre = gu_pre[:, :ff]
    up_pre = gu_pre[:, ff:]
    gate_sigmoid = jax.nn.sigmoid(gate_pre)
    active = gate_pre * gate_sigmoid
    hidden = (active * up_pre).astype(jnp.bfloat16)
    grad_up = (grad_hidden * active).astype(jnp.bfloat16)
    grad_gate = (
        grad_hidden * up_pre * gate_sigmoid * (1.0 + gate_pre * (1.0 - gate_sigmoid))
    ).astype(jnp.bfloat16)

    full_grad = lax.dot_general(
        hidden, upstream, (((0,), (0,)), ((), ())), preferred_element_type=jnp.float32
    )
    cols = full_grad.shape[1] // ndp
    grad_down = lax.dynamic_slice_in_dim(full_grad, j * cols, cols, axis=1)
    for s in range(1, ndp):
        blk = lax.dynamic_slice_in_dim(full_grad, ((j + s) % ndp) * cols, cols, axis=1)
        got = lax.ppermute(blk.astype(jnp.bfloat16), "dp", _shift(ndp, s))
        grad_down = grad_down + got.astype(jnp.float32)

    both = jnp.concatenate([grad_gate, grad_up], axis=1)
    dcols = weights_full.shape[0] // 2
    part_y = lax.dot_general(
        both, weights_full[dcols:], (((1,), (1,)), ((), ())), preferred_element_type=jnp.float32
    ).astype(jnp.bfloat16)
    part_y, both = lax.optimization_barrier((part_y, both))
    part_z = lax.dot_general(
        both, weights_full[:dcols], (((1,), (1,)), ((), ())), preferred_element_type=jnp.float32
    ).astype(jnp.bfloat16)
    input_grad = _ring_reduce_scatter(part_z, part_y)

    first_new = 0.9 * first_moment[0] + 0.1 * grad_down
    second_new = 0.999 * second_moment[0] + 0.001 * grad_down * grad_down
    adam_step = first_new / bias_one / (jnp.sqrt(second_new / bias_two) + 1e-08) + 0.1 * master
    inner_params = master - 0.001 * adam_step
    drift_local = anchor - inner_params

    nout = lax.axis_size("outer")
    total = drift_local.astype(jnp.bfloat16)
    step = 1
    while step < nout:
        perm = [(i, i ^ step) for i in range(nout)]
        mine = total.astype(jnp.bfloat16)
        total = mine.astype(jnp.float32) + lax.ppermute(mine, "outer", perm).astype(jnp.float32)
        step *= 2
    mean_drift = total / nout
    momentum_out = 0.9 * outer_momentum + mean_drift
    new_params = anchor - 0.7 * (mean_drift + 0.9 * momentum_out)
    return (new_params, first_new[None], second_new[None], momentum_out, input_grad[None])


def solution(mesh):
    return jax.shard_map(
        shards,
        mesh=mesh,
        in_specs=(
            P("outer", "dp", None),
            P("outer", "dp", None),
            P("outer", "dp", "mp"),
            P("outer", "dp", "mp"),
            P("outer", "mp", "dp"),
            P("outer", "mp", "dp"),
            P("outer", "mp", "dp"),
            P("mp", "dp"),
            P("mp", "dp"),
        ),
        out_specs=(
            P("mp", "dp"),
            P("outer", "mp", "dp"),
            P("outer", "mp", "dp"),
            P("mp", "dp"),
            P("outer", ("dp", "mp"), None),
        ),
        check_vma=False,
    )
```

```python
import jax
import jax.numpy as jnp
from jax import lax
from jax.sharding import PartitionSpec as P

bias_one = 1.0 - (0.9**50) ** 2
bias_two = 1.0 - (0.999**50) ** 2


def _shift(n, s):
    return [(i, (i + s) % n) for i in range(n)]


def _ring_reduce_scatter(part):
    nmp = lax.axis_size("mp")
    m = lax.axis_index("mp")
    nlo = 2
    nz = nmp // nlo
    far = nz // 2
    z = m // nlo
    lo = m % nlo
    rows = part.shape[0] // nz
    halfc = part.shape[1] // 2
    up = [(i, ((i // nlo + 1) % nz) * nlo + i % nlo) for i in range(nmp)]
    down = [(i, ((i // nlo - 1) % nz) * nlo + i % nlo) for i in range(nmp)]

    def chunk(c):
        return lax.dynamic_slice_in_dim(part, (c % nz) * rows, rows, axis=0).astype(jnp.float32)

    first = chunk(z + far)
    send_a = first[:, :halfc]
    send_b = first[:, halfc:]
    for r in range(2, far + 2):
        got_a = lax.ppermute(send_a.astype(jnp.bfloat16), "mp", up).astype(jnp.float32)
        got_b = lax.ppermute(send_b.astype(jnp.bfloat16), "mp", down).astype(jnp.float32)
        own_a = chunk(z + far + 1 - r)
        own_b = chunk(z - far - 1 + r)
        if r == 2:
            got_a = jnp.concatenate([got_a, jnp.zeros_like(got_a)], axis=1)
            got_b = jnp.concatenate([jnp.zeros_like(got_b), got_b], axis=1)
        if r <= far:
            send_a = got_a + own_a
            send_b = got_b + own_b
    acc = own_a + got_a + got_b
    sub = rows // nlo
    mine = lax.dynamic_slice_in_dim(acc, lo * sub, sub, axis=0)
    other = lax.dynamic_slice_in_dim(acc, (1 - lo) * sub, sub, axis=0)
    got = lax.ppermute(other.astype(jnp.bfloat16), "mp", [(i, i ^ 1) for i in range(nmp)])
    return (mine + got.astype(jnp.float32)).astype(jnp.bfloat16)


def shards(
    tokens,
    cotangent,
    gate_weight,
    up_weight,
    down_master,
    first_moment,
    second_moment,
    anchor,
    outer_momentum,
):
    ndp = lax.axis_size("dp")
    j = lax.axis_index("dp")
    inputs = tokens[0]
    upstream = cotangent[0]
    master = down_master[0]
    down_half = master.astype(jnp.bfloat16)
    ff = master.shape[0]

    assert ndp == 4
    shard = jnp.concatenate([gate_weight[0], up_weight[0], down_half.T], axis=1)
    rows = shard.shape[0]
    half = rows // 2
    from_left = lax.ppermute(shard, "dp", _shift(ndp, 1))
    from_right = lax.ppermute(shard, "dp", _shift(ndp, -1))
    far_a = lax.ppermute(from_left[:half], "dp", _shift(ndp, 1))
    far_b = lax.ppermute(from_right[half:], "dp", _shift(ndp, -1))
    pieces = [
        (j * rows, shard),
        (((j - 1) % ndp) * rows, from_left),
        (((j + 1) % ndp) * rows, from_right),
        (((j + 2) % ndp) * rows, far_a),
        (((j + 2) % ndp) * rows + half, far_b),
    ]

    gu_pre = None
    grad_hidden = None
    weights_full = jnp.zeros((rows * ndp, 2 * ff), jnp.bfloat16)
    for start, piece in pieces:
        size = piece.shape[0]
        xs = lax.dynamic_slice_in_dim(inputs, start, size, axis=1)
        gs = lax.dynamic_slice_in_dim(upstream, start, size, axis=1)
        p1 = jnp.dot(xs, piece[:, : 2 * ff], preferred_element_type=jnp.float32)
        p2 = jnp.dot(gs, piece[:, 2 * ff :], preferred_element_type=jnp.float32)
        gu_pre = p1 if gu_pre is None else gu_pre + p1
        grad_hidden = p2 if grad_hidden is None else grad_hidden + p2
        weights_full = lax.dynamic_update_slice(weights_full, piece[:, : 2 * ff], (start, 0))

    gate_pre = gu_pre[:, :ff]
    up_pre = gu_pre[:, ff:]
    gate_sigmoid = jax.nn.sigmoid(gate_pre)
    active = gate_pre * gate_sigmoid
    hidden = (active * up_pre).astype(jnp.bfloat16)
    grad_up = (grad_hidden * active).astype(jnp.bfloat16)
    grad_gate = (
        grad_hidden * up_pre * gate_sigmoid * (1.0 + gate_pre * (1.0 - gate_sigmoid))
    ).astype(jnp.bfloat16)

    full_grad = jnp.dot(hidden.T, upstream, preferred_element_type=jnp.float32)
    grad_down = lax.psum_scatter(
        full_grad.astype(jnp.bfloat16), "dp", scatter_dimension=1, tiled=True
    ).astype(jnp.float32)

    both = jnp.concatenate([grad_gate, grad_up], axis=1)
    partial_sum = lax.dot_general(
        both, weights_full, (((1,), (1,)), ((), ())), preferred_element_type=jnp.float32
    )
    input_grad = _ring_reduce_scatter(partial_sum.astype(jnp.bfloat16))

    first_new = 0.9 * first_moment[0] + 0.1 * grad_down
    second_new = 0.999 * second_moment[0] + 0.001 * grad_down * grad_down
    adam_step = first_new / bias_one / (jnp.sqrt(second_new / bias_two) + 1e-08) + 0.1 * master
    inner_params = master - 0.001 * adam_step
    drift_local = anchor - inner_params

    nout = lax.axis_size("outer")
    total = drift_local.astype(jnp.bfloat16)
    step = 1
    while step < nout:
        perm = [(i, i ^ step) for i in range(nout)]
        mine = total.astype(jnp.bfloat16)
        total = mine.astype(jnp.float32) + lax.ppermute(mine, "outer", perm).astype(jnp.float32)
        step *= 2
    mean_drift = total / nout
    momentum_out = 0.9 * outer_momentum + mean_drift
    new_params = anchor - 0.7 * (mean_drift + 0.9 * momentum_out)
    return (new_params, first_new[None], second_new[None], momentum_out, input_grad[None])


def solution(mesh):
    return jax.shard_map(
        shards,
        mesh=mesh,
        in_specs=(
            P("outer", "dp", None),
            P("outer", "dp", None),
            P("outer", "dp", "mp"),
            P("outer", "dp", "mp"),
            P("outer", "mp", "dp"),
            P("outer", "mp", "dp"),
            P("outer", "mp", "dp"),
            P("mp", "dp"),
            P("mp", "dp"),
        ),
        out_specs=(
            P("mp", "dp"),
            P("outer", "mp", "dp"),
            P("outer", "mp", "dp"),
            P("mp", "dp"),
            P("outer", ("dp", "mp"), None),
        ),
        check_vma=False,
    )
```

```python
import jax
import jax.numpy as jnp
from jax import lax
from jax.sharding import PartitionSpec as P

bias_one = 1.0 - (0.9**50) ** 2
bias_two = 1.0 - (0.999**50) ** 2


def _shift(n, s):
    return [(i, (i + s) % n) for i in range(n)]


def _z_reduce_scatter(chunks, z, nz, up, down):
    far = nz // 2
    halfc = chunks.shape[2] // 2

    def chunk(c):
        return lax.dynamic_index_in_dim(chunks, c % nz, axis=0, keepdims=False).astype(jnp.float32)

    first = chunk(z + far)
    send_a = first[:, :halfc]
    send_b = first[:, halfc:]
    for r in range(2, far + 2):
        got_a = lax.ppermute(send_a.astype(jnp.bfloat16), "mp", up).astype(jnp.float32)
        got_b = lax.ppermute(send_b.astype(jnp.bfloat16), "mp", down).astype(jnp.float32)
        own_a = chunk(z + far + 1 - r)
        own_b = chunk(z - far - 1 + r)
        if r == 2:
            got_a = jnp.concatenate([got_a, jnp.zeros_like(got_a)], axis=1)
            got_b = jnp.concatenate([jnp.zeros_like(got_b), got_b], axis=1)
        if r <= far:
            send_a = got_a + own_a
            send_b = got_b + own_b
    return own_a + got_a + got_b


def _ring_reduce_scatter(part):
    nmp = lax.axis_size("mp")
    m = lax.axis_index("mp")
    nlo = 2
    nz = nmp // nlo
    z = m // nlo
    lo = m % nlo
    rows = part.shape[0] // nz
    sub = rows // nlo
    halfc = part.shape[1] // 2
    up = [(i, ((i // nlo + 1) % nz) * nlo + i % nlo) for i in range(nmp)]
    down = [(i, ((i // nlo - 1) % nz) * nlo + i % nlo) for i in range(nmp)]
    pa = part[:, :halfc].reshape(nz, rows, halfc)
    pb = part[:, halfc:].reshape(nz, rows, halfc)
    acc = jnp.concatenate(
        [_z_reduce_scatter(pa, z, nz, up, down), _z_reduce_scatter(pb, z, nz, up, down)], axis=1
    )
    mine = lax.dynamic_slice_in_dim(acc, lo * sub, sub, axis=0)
    other = lax.dynamic_slice_in_dim(acc, (1 - lo) * sub, sub, axis=0)
    got = lax.ppermute(other.astype(jnp.bfloat16), "mp", [(i, i ^ 1) for i in range(nmp)])
    return (mine + got.astype(jnp.float32)).astype(jnp.bfloat16)


def shards(
    tokens,
    cotangent,
    gate_weight,
    up_weight,
    down_master,
    first_moment,
    second_moment,
    anchor,
    outer_momentum,
):
    ndp = lax.axis_size("dp")
    j = lax.axis_index("dp")
    inputs = tokens[0]
    upstream = cotangent[0]
    master = down_master[0]
    down_half = master.astype(jnp.bfloat16)
    ff = master.shape[0]

    assert ndp == 4
    shard = jnp.concatenate([gate_weight[0], up_weight[0], down_half.T], axis=1)
    rows = shard.shape[0]
    half = rows // 2
    from_left = lax.ppermute(shard, "dp", _shift(ndp, 1))
    from_right = lax.ppermute(shard, "dp", _shift(ndp, -1))
    far_a = lax.ppermute(from_left[:half], "dp", _shift(ndp, 1))
    far_b = lax.ppermute(from_right[half:], "dp", _shift(ndp, -1))
    pieces = [
        (j * rows, shard),
        (((j - 1) % ndp) * rows, from_left),
        (((j + 1) % ndp) * rows, from_right),
        (((j + 2) % ndp) * rows, far_a),
        (((j + 2) % ndp) * rows + half, far_b),
    ]

    gu_pre = None
    grad_hidden = None
    weights_full = jnp.zeros((rows * ndp, 2 * ff), jnp.bfloat16)
    for start, piece in pieces:
        size = piece.shape[0]
        xs = lax.dynamic_slice_in_dim(inputs, start, size, axis=1)
        gs = lax.dynamic_slice_in_dim(upstream, start, size, axis=1)
        p1 = jnp.dot(xs, piece[:, : 2 * ff], preferred_element_type=jnp.float32)
        p2 = jnp.dot(gs, piece[:, 2 * ff :], preferred_element_type=jnp.float32)
        gu_pre = p1 if gu_pre is None else gu_pre + p1
        grad_hidden = p2 if grad_hidden is None else grad_hidden + p2
        weights_full = lax.dynamic_update_slice(weights_full, piece[:, : 2 * ff], (start, 0))

    gate_pre = gu_pre[:, :ff]
    up_pre = gu_pre[:, ff:]
    gate_sigmoid = jax.nn.sigmoid(gate_pre)
    active = gate_pre * gate_sigmoid
    hidden = (active * up_pre).astype(jnp.bfloat16)
    grad_up = (grad_hidden * active).astype(jnp.bfloat16)
    grad_gate = (
        grad_hidden * up_pre * gate_sigmoid * (1.0 + gate_pre * (1.0 - gate_sigmoid))
    ).astype(jnp.bfloat16)

    full_grad = lax.dot_general(
        hidden, upstream, (((0,), (0,)), ((), ())), preferred_element_type=jnp.float32
    )
    cols = full_grad.shape[1] // ndp
    grad_down = lax.dynamic_slice_in_dim(full_grad, j * cols, cols, axis=1)
    for s in range(1, ndp):
        blk = lax.dynamic_slice_in_dim(full_grad, ((j + s) % ndp) * cols, cols, axis=1)
        got = lax.ppermute(blk.astype(jnp.bfloat16), "dp", _shift(ndp, s))
        grad_down = grad_down + got.astype(jnp.float32)

    both = jnp.concatenate([grad_gate, grad_up], axis=1)
    partial_sum = lax.dot_general(
        both, weights_full, (((1,), (1,)), ((), ())), preferred_element_type=jnp.float32
    )
    input_grad = _ring_reduce_scatter(partial_sum.astype(jnp.bfloat16))

    first_new = 0.9 * first_moment[0] + 0.1 * grad_down
    second_new = 0.999 * second_moment[0] + 0.001 * grad_down * grad_down
    adam_step = first_new / bias_one / (jnp.sqrt(second_new / bias_two) + 1e-08) + 0.1 * master
    inner_params = master - 0.001 * adam_step
    drift_local = anchor - inner_params

    nout = lax.axis_size("outer")
    total = drift_local.astype(jnp.bfloat16)
    step = 1
    while step < nout:
        perm = [(i, i ^ step) for i in range(nout)]
        mine = total.astype(jnp.bfloat16)
        total = mine.astype(jnp.float32) + lax.ppermute(mine, "outer", perm).astype(jnp.float32)
        step *= 2
    mean_drift = total / nout
    momentum_out = 0.9 * outer_momentum + mean_drift
    new_params = anchor - 0.7 * (mean_drift + 0.9 * momentum_out)
    return (new_params, first_new[None], second_new[None], momentum_out, input_grad[None])


def solution(mesh):
    return jax.shard_map(
        shards,
        mesh=mesh,
        in_specs=(
            P("outer", "dp", None),
            P("outer", "dp", None),
            P("outer", "dp", "mp"),
            P("outer", "dp", "mp"),
            P("outer", "mp", "dp"),
            P("outer", "mp", "dp"),
            P("outer", "mp", "dp"),
            P("mp", "dp"),
            P("mp", "dp"),
        ),
        out_specs=(
            P("mp", "dp"),
            P("outer", "mp", "dp"),
            P("outer", "mp", "dp"),
            P("mp", "dp"),
            P("outer", ("dp", "mp"), None),
        ),
        check_vma=False,
    )
```

```python
import jax
import jax.numpy as jnp
from jax import lax
from jax.sharding import PartitionSpec as P

bias_one = 1.0 - (0.9**50) ** 2
bias_two = 1.0 - (0.999**50) ** 2


def _shift(n, s):
    return [(i, (i + s) % n) for i in range(n)]


def _z_reduce_scatter(chunks, z, nz, up, down):
    far = nz // 2
    halfc = chunks.shape[2] // 2

    def chunk(c):
        return lax.dynamic_index_in_dim(chunks, c % nz, axis=0, keepdims=False).astype(jnp.float32)

    first = chunk(z + far)
    send_a = first[:, :halfc]
    send_b = first[:, halfc:]
    for r in range(2, far + 2):
        got_a = lax.ppermute(send_a.astype(jnp.bfloat16), "mp", up).astype(jnp.float32)
        got_b = lax.ppermute(send_b.astype(jnp.bfloat16), "mp", down).astype(jnp.float32)
        own_a = chunk(z + far + 1 - r)
        own_b = chunk(z - far - 1 + r)
        if r == 2:
            got_a = jnp.concatenate([got_a, jnp.zeros_like(got_a)], axis=1)
            got_b = jnp.concatenate([jnp.zeros_like(got_b), got_b], axis=1)
        if r <= far:
            send_a = got_a + own_a
            send_b = got_b + own_b
    return own_a + got_a + got_b


def _ring_reduce_scatter(part, sync):
    nmp = lax.axis_size("mp")
    m = lax.axis_index("mp")
    nlo = 2
    nz = nmp // nlo
    z = m // nlo
    lo = m % nlo
    rows = part.shape[0] // nz
    sub = rows // nlo
    halfc = part.shape[1] // 2
    up = [(i, ((i // nlo + 1) % nz) * nlo + i % nlo) for i in range(nmp)]
    down = [(i, ((i // nlo - 1) % nz) * nlo + i % nlo) for i in range(nmp)]
    pa = part[:, :halfc].reshape(nz, rows, halfc)
    pb = part[:, halfc:].reshape(nz, rows, halfc)
    acc = jnp.concatenate(
        [_z_reduce_scatter(pa, z, nz, up, down), _z_reduce_scatter(pb, z, nz, up, down)], axis=1
    )
    mine = lax.dynamic_slice_in_dim(acc, lo * sub, sub, axis=0)
    other = lax.dynamic_slice_in_dim(acc, (1 - lo) * sub, sub, axis=0)
    other, sync = lax.optimization_barrier((other, sync))
    got = lax.ppermute(other.astype(jnp.bfloat16), "mp", [(i, i ^ 1) for i in range(nmp)])
    return (mine + got.astype(jnp.float32)).astype(jnp.bfloat16), sync


def shards(
    tokens,
    cotangent,
    gate_weight,
    up_weight,
    down_master,
    first_moment,
    second_moment,
    anchor,
    outer_momentum,
):
    ndp = lax.axis_size("dp")
    j = lax.axis_index("dp")
    inputs = tokens[0]
    upstream = cotangent[0]
    master = down_master[0]
    down_half = master.astype(jnp.bfloat16)
    ff = master.shape[0]

    assert ndp == 4
    shard = jnp.concatenate([gate_weight[0], up_weight[0], down_half.T], axis=1)
    rows = shard.shape[0]
    half = rows // 2
    from_left = lax.ppermute(shard, "dp", _shift(ndp, 1))
    from_right = lax.ppermute(shard, "dp", _shift(ndp, -1))
    far_a = lax.ppermute(from_left[:half], "dp", _shift(ndp, 1))
    far_b = lax.ppermute(from_right[half:], "dp", _shift(ndp, -1))
    pieces = [
        (j * rows, shard),
        (((j - 1) % ndp) * rows, from_left),
        (((j + 1) % ndp) * rows, from_right),
        (((j + 2) % ndp) * rows, far_a),
        (((j + 2) % ndp) * rows + half, far_b),
    ]

    gu_pre = None
    grad_hidden = None
    weights_full = jnp.zeros((rows * ndp, 2 * ff), jnp.bfloat16)
    for start, piece in pieces:
        size = piece.shape[0]
        xs = lax.dynamic_slice_in_dim(inputs, start, size, axis=1)
        gs = lax.dynamic_slice_in_dim(upstream, start, size, axis=1)
        p1 = jnp.dot(xs, piece[:, : 2 * ff], preferred_element_type=jnp.float32)
        p2 = jnp.dot(gs, piece[:, 2 * ff :], preferred_element_type=jnp.float32)
        gu_pre = p1 if gu_pre is None else gu_pre + p1
        grad_hidden = p2 if grad_hidden is None else grad_hidden + p2
        weights_full = lax.dynamic_update_slice(weights_full, piece[:, : 2 * ff], (start, 0))

    gate_pre = gu_pre[:, :ff]
    up_pre = gu_pre[:, ff:]
    gate_sigmoid = jax.nn.sigmoid(gate_pre)
    active = gate_pre * gate_sigmoid
    hidden = (active * up_pre).astype(jnp.bfloat16)
    grad_up = (grad_hidden * active).astype(jnp.bfloat16)
    grad_gate = (
        grad_hidden * up_pre * gate_sigmoid * (1.0 + gate_pre * (1.0 - gate_sigmoid))
    ).astype(jnp.bfloat16)

    full_grad = lax.dot_general(
        hidden, upstream, (((0,), (0,)), ((), ())), preferred_element_type=jnp.float32
    )
    cols = full_grad.shape[1] // ndp
    grad_down = lax.dynamic_slice_in_dim(full_grad, j * cols, cols, axis=1)
    for s in range(1, ndp):
        blk = lax.dynamic_slice_in_dim(full_grad, ((j + s) % ndp) * cols, cols, axis=1)
        got = lax.ppermute(blk.astype(jnp.bfloat16), "dp", _shift(ndp, s))
        grad_down = grad_down + got.astype(jnp.float32)

    both = jnp.concatenate([grad_gate, grad_up], axis=1)
    partial_sum = lax.dot_general(
        both, weights_full, (((1,), (1,)), ((), ())), preferred_element_type=jnp.float32
    )

    first_new = 0.9 * first_moment[0] + 0.1 * grad_down
    second_new = 0.999 * second_moment[0] + 0.001 * grad_down * grad_down
    adam_step = first_new / bias_one / (jnp.sqrt(second_new / bias_two) + 1e-08) + 0.1 * master
    inner_params = master - 0.001 * adam_step
    drift_local = anchor - inner_params

    nout = lax.axis_size("outer")
    total = drift_local.astype(jnp.bfloat16)
    step = 1
    while step < nout:
        perm = [(i, i ^ step) for i in range(nout)]
        mine = total.astype(jnp.bfloat16)
        total = mine.astype(jnp.float32) + lax.ppermute(mine, "outer", perm).astype(jnp.float32)
        step *= 2
    input_grad, total = _ring_reduce_scatter(partial_sum.astype(jnp.bfloat16), total)
    mean_drift = total / nout
    momentum_out = 0.9 * outer_momentum + mean_drift
    new_params = anchor - 0.7 * (mean_drift + 0.9 * momentum_out)
    return (new_params, first_new[None], second_new[None], momentum_out, input_grad[None])


def solution(mesh):
    return jax.shard_map(
        shards,
        mesh=mesh,
        in_specs=(
            P("outer", "dp", None),
            P("outer", "dp", None),
            P("outer", "dp", "mp"),
            P("outer", "dp", "mp"),
            P("outer", "mp", "dp"),
            P("outer", "mp", "dp"),
            P("outer", "mp", "dp"),
            P("mp", "dp"),
            P("mp", "dp"),
        ),
        out_specs=(
            P("mp", "dp"),
            P("outer", "mp", "dp"),
            P("outer", "mp", "dp"),
            P("mp", "dp"),
            P("outer", ("dp", "mp"), None),
        ),
        check_vma=False,
    )
```

```python
import jax
import jax.numpy as jnp
from jax import lax
from jax.sharding import PartitionSpec as P

bias_one = 1.0 - (0.9**50) ** 2
bias_two = 1.0 - (0.999**50) ** 2


def _shift(n, s):
    return [(i, (i + s) % n) for i in range(n)]


def _z_reduce_scatter(chunks, z, nz, up, down):
    far = nz // 2
    halfc = chunks.shape[2] // 2

    def chunk(c):
        return lax.dynamic_index_in_dim(chunks, c % nz, axis=0, keepdims=False).astype(jnp.float32)

    first = chunk(z + far)
    send_a = first[:, :halfc]
    send_b = first[:, halfc:]
    for r in range(2, far + 2):
        got_a = lax.ppermute(send_a.astype(jnp.bfloat16), "mp", up).astype(jnp.float32)
        got_b = lax.ppermute(send_b.astype(jnp.bfloat16), "mp", down).astype(jnp.float32)
        own_a = chunk(z + far + 1 - r)
        own_b = chunk(z - far - 1 + r)
        if r == 2:
            got_a = jnp.concatenate([got_a, jnp.zeros_like(got_a)], axis=1)
            got_b = jnp.concatenate([jnp.zeros_like(got_b), got_b], axis=1)
        if r <= far:
            send_a = got_a + own_a
            send_b = got_b + own_b
    return own_a + got_a + got_b


def _ring_reduce_scatter(part, sync):
    nmp = lax.axis_size("mp")
    m = lax.axis_index("mp")
    nlo = 2
    nz = nmp // nlo
    z = m // nlo
    lo = m % nlo
    rows = part.shape[0] // nz
    sub = rows // nlo
    halfc = part.shape[1] // 2
    up = [(i, ((i // nlo + 1) % nz) * nlo + i % nlo) for i in range(nmp)]
    down = [(i, ((i // nlo - 1) % nz) * nlo + i % nlo) for i in range(nmp)]
    pa = part[:, :halfc].reshape(nz, rows, halfc)
    pb = part[:, halfc:].reshape(nz, rows, halfc)
    acc = jnp.concatenate(
        [_z_reduce_scatter(pa, z, nz, up, down), _z_reduce_scatter(pb, z, nz, up, down)], axis=1
    )
    mine = lax.dynamic_slice_in_dim(acc, lo * sub, sub, axis=0)
    other = lax.dynamic_slice_in_dim(acc, (1 - lo) * sub, sub, axis=0)
    other, sync = lax.optimization_barrier((other, sync))
    got = lax.ppermute(other.astype(jnp.bfloat16), "mp", [(i, i ^ 1) for i in range(nmp)])
    return (mine + got.astype(jnp.float32)).astype(jnp.bfloat16), sync


def shards(
    tokens,
    cotangent,
    gate_weight,
    up_weight,
    down_master,
    first_moment,
    second_moment,
    anchor,
    outer_momentum,
):
    ndp = lax.axis_size("dp")
    j = lax.axis_index("dp")
    inputs = tokens[0]
    upstream = cotangent[0]
    master = down_master[0]
    down_half = master.astype(jnp.bfloat16)
    ff = master.shape[0]

    assert ndp == 4
    shard = jnp.concatenate([gate_weight[0], up_weight[0], down_half.T], axis=1)
    rows = shard.shape[0]
    half = rows // 2
    from_left = lax.ppermute(shard, "dp", _shift(ndp, 1))
    from_right = lax.ppermute(shard, "dp", _shift(ndp, -1))
    far_a = lax.ppermute(from_left[:half], "dp", _shift(ndp, 1))
    far_b = lax.ppermute(from_right[half:], "dp", _shift(ndp, -1))
    pieces = [
        (j * rows, shard),
        (((j - 1) % ndp) * rows, from_left),
        (((j + 1) % ndp) * rows, from_right),
        (((j + 2) % ndp) * rows, far_a),
        (((j + 2) % ndp) * rows + half, far_b),
    ]

    gu_pre = None
    grad_hidden = None
    weights_full = jnp.zeros((rows * ndp, 2 * ff), jnp.bfloat16)
    for start, piece in pieces:
        size = piece.shape[0]
        xs = lax.dynamic_slice_in_dim(inputs, start, size, axis=1)
        gs = lax.dynamic_slice_in_dim(upstream, start, size, axis=1)
        p1 = jnp.dot(xs, piece[:, : 2 * ff], preferred_element_type=jnp.float32)
        p2 = jnp.dot(gs, piece[:, 2 * ff :], preferred_element_type=jnp.float32)
        gu_pre = p1 if gu_pre is None else gu_pre + p1
        grad_hidden = p2 if grad_hidden is None else grad_hidden + p2
        weights_full = lax.dynamic_update_slice(weights_full, piece[:, : 2 * ff], (start, 0))

    gate_pre = gu_pre[:, :ff]
    up_pre = gu_pre[:, ff:]
    gate_sigmoid = jax.nn.sigmoid(gate_pre)
    active = gate_pre * gate_sigmoid
    hidden = (active * up_pre).astype(jnp.bfloat16)
    grad_up = (grad_hidden * active).astype(jnp.bfloat16)
    grad_gate = (
        grad_hidden * up_pre * gate_sigmoid * (1.0 + gate_pre * (1.0 - gate_sigmoid))
    ).astype(jnp.bfloat16)

    full_grad = lax.dot_general(
        hidden, upstream, (((0,), (0,)), ((), ())), preferred_element_type=jnp.float32
    )
    cols = full_grad.shape[1] // ndp
    blocks = full_grad.astype(jnp.bfloat16).reshape(full_grad.shape[0], ndp, cols)
    got = lax.all_to_all(blocks, "dp", 1, 1, tiled=True)
    grad_down = jnp.sum(got.astype(jnp.float32), axis=1)

    both = jnp.concatenate([grad_gate, grad_up], axis=1)
    partial_sum = lax.dot_general(
        both, weights_full, (((1,), (1,)), ((), ())), preferred_element_type=jnp.float32
    )

    first_new = 0.9 * first_moment[0] + 0.1 * grad_down
    second_new = 0.999 * second_moment[0] + 0.001 * grad_down * grad_down
    adam_step = first_new / bias_one / (jnp.sqrt(second_new / bias_two) + 1e-08) + 0.1 * master
    inner_params = master - 0.001 * adam_step
    drift_local = anchor - inner_params

    nout = lax.axis_size("outer")
    total = drift_local.astype(jnp.bfloat16)
    step = 1
    while step < nout:
        perm = [(i, i ^ step) for i in range(nout)]
        mine = total.astype(jnp.bfloat16)
        total = mine.astype(jnp.float32) + lax.ppermute(mine, "outer", perm).astype(jnp.float32)
        step *= 2
    input_grad, total = _ring_reduce_scatter(partial_sum.astype(jnp.bfloat16), total)
    mean_drift = total / nout
    momentum_out = 0.9 * outer_momentum + mean_drift
    new_params = anchor - 0.7 * (mean_drift + 0.9 * momentum_out)
    return (new_params, first_new[None], second_new[None], momentum_out, input_grad[None])


def solution(mesh):
    return jax.shard_map(
        shards,
        mesh=mesh,
        in_specs=(
            P("outer", "dp", None),
            P("outer", "dp", None),
            P("outer", "dp", "mp"),
            P("outer", "dp", "mp"),
            P("outer", "mp", "dp"),
            P("outer", "mp", "dp"),
            P("outer", "mp", "dp"),
            P("mp", "dp"),
            P("mp", "dp"),
        ),
        out_specs=(
            P("mp", "dp"),
            P("outer", "mp", "dp"),
            P("outer", "mp", "dp"),
            P("mp", "dp"),
            P("outer", ("dp", "mp"), None),
        ),
        check_vma=False,
    )
```

```python
import jax
import jax.numpy as jnp
from jax import lax
from jax.sharding import PartitionSpec as P

bias_one = 1.0 - (0.9**50) ** 2
bias_two = 1.0 - (0.999**50) ** 2


def _shift(n, s):
    return [(i, (i + s) % n) for i in range(n)]


def _z_reduce_scatter(chunks, z, nz, up, down):
    far = nz // 2
    halfc = chunks.shape[2] // 2

    def chunk(c):
        return lax.dynamic_index_in_dim(chunks, c % nz, axis=0, keepdims=False).astype(jnp.float32)

    first = chunk(z + far)
    send_a = first[:, :halfc]
    send_b = first[:, halfc:]
    for r in range(2, far + 2):
        got_a = lax.ppermute(send_a.astype(jnp.bfloat16), "mp", up).astype(jnp.float32)
        got_b = lax.ppermute(send_b.astype(jnp.bfloat16), "mp", down).astype(jnp.float32)
        own_a = chunk(z + far + 1 - r)
        own_b = chunk(z - far - 1 + r)
        if r == 2:
            got_a = jnp.concatenate([got_a, jnp.zeros_like(got_a)], axis=1)
            got_b = jnp.concatenate([jnp.zeros_like(got_b), got_b], axis=1)
        if r <= far:
            send_a = got_a + own_a
            send_b = got_b + own_b
    return own_a + got_a + got_b


def _ring_reduce_scatter(part, sync):
    nmp = lax.axis_size("mp")
    m = lax.axis_index("mp")
    nlo = 2
    nz = nmp // nlo
    z = m // nlo
    lo = m % nlo
    rows = part.shape[0] // nz
    sub = rows // nlo
    halfc = part.shape[1] // 2
    up = [(i, ((i // nlo + 1) % nz) * nlo + i % nlo) for i in range(nmp)]
    down = [(i, ((i // nlo - 1) % nz) * nlo + i % nlo) for i in range(nmp)]
    pair = [(i, i ^ 1) for i in range(nmp)]
    outs = []
    for h in range(2):
        ph = part[:, h * halfc : (h + 1) * halfc].reshape(nz, rows, halfc)
        acc = _z_reduce_scatter(ph, z, nz, up, down)
        mine = lax.dynamic_slice_in_dim(acc, lo * sub, sub, axis=0)
        other = lax.dynamic_slice_in_dim(acc, (1 - lo) * sub, sub, axis=0)
        if h == 1:
            other, sync = lax.optimization_barrier((other, sync))
        got = lax.ppermute(other.astype(jnp.bfloat16), "mp", pair)
        outs.append(mine + got.astype(jnp.float32))
    return jnp.concatenate(outs, axis=1).astype(jnp.bfloat16), sync


def shards(
    tokens,
    cotangent,
    gate_weight,
    up_weight,
    down_master,
    first_moment,
    second_moment,
    anchor,
    outer_momentum,
):
    ndp = lax.axis_size("dp")
    j = lax.axis_index("dp")
    inputs = tokens[0]
    upstream = cotangent[0]
    master = down_master[0]
    down_half = master.astype(jnp.bfloat16)
    ff = master.shape[0]

    assert ndp == 4
    shard = jnp.concatenate([gate_weight[0], up_weight[0], down_half.T], axis=1)
    rows = shard.shape[0]
    half = rows // 2
    from_left = lax.ppermute(shard, "dp", _shift(ndp, 1))
    from_right = lax.ppermute(shard, "dp", _shift(ndp, -1))
    far_a = lax.ppermute(from_left[:half], "dp", _shift(ndp, 1))
    far_b = lax.ppermute(from_right[half:], "dp", _shift(ndp, -1))
    pieces = [
        (j * rows, shard),
        (((j - 1) % ndp) * rows, from_left),
        (((j + 1) % ndp) * rows, from_right),
        (((j + 2) % ndp) * rows, far_a),
        (((j + 2) % ndp) * rows + half, far_b),
    ]

    gu_pre = None
    grad_hidden = None
    weights_full = jnp.zeros((rows * ndp, 2 * ff), jnp.bfloat16)
    for start, piece in pieces:
        size = piece.shape[0]
        xs = lax.dynamic_slice_in_dim(inputs, start, size, axis=1)
        gs = lax.dynamic_slice_in_dim(upstream, start, size, axis=1)
        p1 = jnp.dot(xs, piece[:, : 2 * ff], preferred_element_type=jnp.float32)
        p2 = jnp.dot(gs, piece[:, 2 * ff :], preferred_element_type=jnp.float32)
        gu_pre = p1 if gu_pre is None else gu_pre + p1
        grad_hidden = p2 if grad_hidden is None else grad_hidden + p2
        weights_full = lax.dynamic_update_slice(weights_full, piece[:, : 2 * ff], (start, 0))

    gate_pre = gu_pre[:, :ff]
    up_pre = gu_pre[:, ff:]
    gate_sigmoid = jax.nn.sigmoid(gate_pre)
    active = gate_pre * gate_sigmoid
    hidden = (active * up_pre).astype(jnp.bfloat16)
    grad_up = (grad_hidden * active).astype(jnp.bfloat16)
    grad_gate = (
        grad_hidden * up_pre * gate_sigmoid * (1.0 + gate_pre * (1.0 - gate_sigmoid))
    ).astype(jnp.bfloat16)

    full_grad = lax.dot_general(
        hidden, upstream, (((0,), (0,)), ((), ())), preferred_element_type=jnp.float32
    )
    cols = full_grad.shape[1] // ndp
    grad_down = lax.dynamic_slice_in_dim(full_grad, j * cols, cols, axis=1)
    for s in range(1, ndp):
        blk = lax.dynamic_slice_in_dim(full_grad, ((j + s) % ndp) * cols, cols, axis=1)
        got = lax.ppermute(blk.astype(jnp.bfloat16), "dp", _shift(ndp, s))
        grad_down = grad_down + got.astype(jnp.float32)

    both = jnp.concatenate([grad_gate, grad_up], axis=1)
    partial_sum = lax.dot_general(
        both, weights_full, (((1,), (1,)), ((), ())), preferred_element_type=jnp.float32
    )

    first_new = 0.9 * first_moment[0] + 0.1 * grad_down
    second_new = 0.999 * second_moment[0] + 0.001 * grad_down * grad_down
    adam_step = first_new / bias_one / (jnp.sqrt(second_new / bias_two) + 1e-08) + 0.1 * master
    inner_params = master - 0.001 * adam_step
    drift_local = anchor - inner_params

    nout = lax.axis_size("outer")
    total = drift_local.astype(jnp.bfloat16)
    step = 1
    while step < nout:
        perm = [(i, i ^ step) for i in range(nout)]
        mine = total.astype(jnp.bfloat16)
        total = mine.astype(jnp.float32) + lax.ppermute(mine, "outer", perm).astype(jnp.float32)
        step *= 2
    input_grad, total = _ring_reduce_scatter(partial_sum.astype(jnp.bfloat16), total)
    mean_drift = total / nout
    momentum_out = 0.9 * outer_momentum + mean_drift
    new_params = anchor - 0.7 * (mean_drift + 0.9 * momentum_out)
    return (new_params, first_new[None], second_new[None], momentum_out, input_grad[None])


def solution(mesh):
    return jax.shard_map(
        shards,
        mesh=mesh,
        in_specs=(
            P("outer", "dp", None),
            P("outer", "dp", None),
            P("outer", "dp", "mp"),
            P("outer", "dp", "mp"),
            P("outer", "mp", "dp"),
            P("outer", "mp", "dp"),
            P("outer", "mp", "dp"),
            P("mp", "dp"),
            P("mp", "dp"),
        ),
        out_specs=(
            P("mp", "dp"),
            P("outer", "mp", "dp"),
            P("outer", "mp", "dp"),
            P("mp", "dp"),
            P("outer", ("dp", "mp"), None),
        ),
        check_vma=False,
    )
```

```python
import jax
import jax.numpy as jnp
from jax import lax
from jax.sharding import PartitionSpec as P

bias_one = 1.0 - (0.9**50) ** 2
bias_two = 1.0 - (0.999**50) ** 2


def _shift(n, s):
    return [(i, (i + s) % n) for i in range(n)]


def _z_reduce_scatter(chunks, z, nz, up, down):
    far = nz // 2
    halfc = chunks.shape[2] // 2

    def chunk(c):
        return lax.dynamic_index_in_dim(chunks, c % nz, axis=0, keepdims=False).astype(jnp.float32)

    first = chunk(z + far)
    send_a = first[:, :halfc]
    send_b = first[:, halfc:]
    for r in range(2, far + 2):
        got_a = lax.ppermute(send_a.astype(jnp.bfloat16), "mp", up).astype(jnp.float32)
        got_b = lax.ppermute(send_b.astype(jnp.bfloat16), "mp", down).astype(jnp.float32)
        own_a = chunk(z + far + 1 - r)
        own_b = chunk(z - far - 1 + r)
        if r == 2:
            got_a = jnp.concatenate([got_a, jnp.zeros_like(got_a)], axis=1)
            got_b = jnp.concatenate([jnp.zeros_like(got_b), got_b], axis=1)
        if r <= far:
            send_a = got_a + own_a
            send_b = got_b + own_b
    return own_a + got_a + got_b


def _ring_reduce_scatter(part, sync):
    nmp = lax.axis_size("mp")
    m = lax.axis_index("mp")
    nlo = 2
    nz = nmp // nlo
    z = m // nlo
    lo = m % nlo
    rows = part.shape[0] // nz
    sub = rows // nlo
    halfc = part.shape[1] // 2
    up = [(i, ((i // nlo + 1) % nz) * nlo + i % nlo) for i in range(nmp)]
    down = [(i, ((i // nlo - 1) % nz) * nlo + i % nlo) for i in range(nmp)]
    pa = part[:, :halfc].reshape(nz, rows, halfc)
    pb = part[:, halfc:].reshape(nz, rows, halfc)
    acc = jnp.concatenate(
        [_z_reduce_scatter(pa, z, nz, up, down), _z_reduce_scatter(pb, z, nz, up, down)], axis=1
    )
    mine = lax.dynamic_slice_in_dim(acc, lo * sub, sub, axis=0)
    other = lax.dynamic_slice_in_dim(acc, (1 - lo) * sub, sub, axis=0)
    other, sync = lax.optimization_barrier((other, sync))
    got = lax.ppermute(other.astype(jnp.bfloat16), "mp", [(i, i ^ 1) for i in range(nmp)])
    return (mine + got.astype(jnp.float32)).astype(jnp.bfloat16), sync


def shards(
    tokens,
    cotangent,
    gate_weight,
    up_weight,
    down_master,
    first_moment,
    second_moment,
    anchor,
    outer_momentum,
):
    ndp = lax.axis_size("dp")
    j = lax.axis_index("dp")
    inputs = tokens[0]
    upstream = cotangent[0]
    master = down_master[0]
    down_half = master.astype(jnp.bfloat16)
    ff = master.shape[0]

    assert ndp == 4
    rows = gate_weight.shape[1]
    dcols = down_half.shape[1]
    shard = jnp.concatenate(
        [gate_weight[0], up_weight[0], down_half.reshape(rows, -1)], axis=1
    )
    half = rows // 2
    from_left = lax.ppermute(shard, "dp", _shift(ndp, 1))
    from_right = lax.ppermute(shard, "dp", _shift(ndp, -1))
    far_a = lax.ppermute(from_left[:half], "dp", _shift(ndp, 1))
    far_b = lax.ppermute(from_right[half:], "dp", _shift(ndp, -1))

    def down_of(piece):
        return piece[:, 2 * ff :].reshape(-1, dcols)

    far = (j + 2) % ndp
    gu_pieces = [
        (j * rows, shard[:, : 2 * ff]),
        (((j - 1) % ndp) * rows, from_left[:, : 2 * ff]),
        (((j + 1) % ndp) * rows, from_right[:, : 2 * ff]),
        (far * rows, far_a[:, : 2 * ff]),
        (far * rows + half, far_b[:, : 2 * ff]),
    ]
    down_pieces = [
        (j * rows, down_half),
        (((j - 1) % ndp) * rows, down_of(from_left)),
        (((j + 1) % ndp) * rows, down_of(from_right)),
        (far * rows, jnp.concatenate([down_of(far_a), down_of(far_b)], axis=0)),
    ]

    gu_pre = None
    grad_hidden = None
    weights_full = jnp.zeros((rows * ndp, 2 * ff), jnp.bfloat16)
    for start, piece in gu_pieces:
        xs = lax.dynamic_slice_in_dim(inputs, start, piece.shape[0], axis=1)
        p1 = jnp.dot(xs, piece, preferred_element_type=jnp.float32)
        gu_pre = p1 if gu_pre is None else gu_pre + p1
        weights_full = lax.dynamic_update_slice(weights_full, piece, (start, 0))
    for start, piece in down_pieces:
        gs = lax.dynamic_slice_in_dim(upstream, start, piece.shape[1], axis=1)
        p2 = lax.dot_general(
            gs, piece, (((1,), (1,)), ((), ())), preferred_element_type=jnp.float32
        )
        grad_hidden = p2 if grad_hidden is None else grad_hidden + p2

    gate_pre = gu_pre[:, :ff]
    up_pre = gu_pre[:, ff:]
    gate_sigmoid = jax.nn.sigmoid(gate_pre)
    active = gate_pre * gate_sigmoid
    hidden = (active * up_pre).astype(jnp.bfloat16)
    grad_up = (grad_hidden * active).astype(jnp.bfloat16)
    grad_gate = (
        grad_hidden * up_pre * gate_sigmoid * (1.0 + gate_pre * (1.0 - gate_sigmoid))
    ).astype(jnp.bfloat16)

    full_grad = lax.dot_general(
        hidden, upstream, (((0,), (0,)), ((), ())), preferred_element_type=jnp.float32
    )
    cols = full_grad.shape[1] // ndp
    grad_down = lax.dynamic_slice_in_dim(full_grad, j * cols, cols, axis=1)
    for s in range(1, ndp):
        blk = lax.dynamic_slice_in_dim(full_grad, ((j + s) % ndp) * cols, cols, axis=1)
        got = lax.ppermute(blk.astype(jnp.bfloat16), "dp", _shift(ndp, s))
        grad_down = grad_down + got.astype(jnp.float32)

    both = jnp.concatenate([grad_gate, grad_up], axis=1)
    partial_sum = lax.dot_general(
        both, weights_full, (((1,), (1,)), ((), ())), preferred_element_type=jnp.float32
    )

    first_new = 0.9 * first_moment[0] + 0.1 * grad_down
    second_new = 0.999 * second_moment[0] + 0.001 * grad_down * grad_down
    adam_step = first_new / bias_one / (jnp.sqrt(second_new / bias_two) + 1e-08) + 0.1 * master
    inner_params = master - 0.001 * adam_step
    drift_local = anchor - inner_params

    nout = lax.axis_size("outer")
    total = drift_local.astype(jnp.bfloat16)
    step = 1
    while step < nout:
        perm = [(i, i ^ step) for i in range(nout)]
        mine = total.astype(jnp.bfloat16)
        total = mine.astype(jnp.float32) + lax.ppermute(mine, "outer", perm).astype(jnp.float32)
        step *= 2
    input_grad, total = _ring_reduce_scatter(partial_sum.astype(jnp.bfloat16), total)
    mean_drift = total / nout
    momentum_out = 0.9 * outer_momentum + mean_drift
    new_params = anchor - 0.7 * (mean_drift + 0.9 * momentum_out)
    return (new_params, first_new[None], second_new[None], momentum_out, input_grad[None])


def solution(mesh):
    return jax.shard_map(
        shards,
        mesh=mesh,
        in_specs=(
            P("outer", "dp", None),
            P("outer", "dp", None),
            P("outer", "dp", "mp"),
            P("outer", "dp", "mp"),
            P("outer", "mp", "dp"),
            P("outer", "mp", "dp"),
            P("outer", "mp", "dp"),
            P("mp", "dp"),
            P("mp", "dp"),
        ),
        out_specs=(
            P("mp", "dp"),
            P("outer", "mp", "dp"),
            P("outer", "mp", "dp"),
            P("mp", "dp"),
            P("outer", ("dp", "mp"), None),
        ),
        check_vma=False,
    )
```

```python
import jax
import jax.numpy as jnp
from jax import lax
from jax.sharding import PartitionSpec as P

bias_one = 1.0 - (0.9**50) ** 2
bias_two = 1.0 - (0.999**50) ** 2


def _shift(n, s):
    return [(i, (i + s) % n) for i in range(n)]


def _z_reduce_scatter(chunks, z, nz, up, down):
    far = nz // 2

    def chunk(c):
        return lax.dynamic_index_in_dim(chunks, c % nz, axis=0, keepdims=False).astype(jnp.float32)

    send_a = chunk(z + far)
    send_b = None
    for r in range(1, far + 1):
        got_a = lax.ppermute(send_a.astype(jnp.bfloat16), "mp", up).astype(jnp.float32)
        got_b = None
        if send_b is not None:
            got_b = lax.ppermute(send_b.astype(jnp.bfloat16), "mp", down).astype(jnp.float32)
        if r < far:
            send_a = got_a + chunk(z + far - r)
            own_b = chunk(z - far + r)
            send_b = own_b if got_b is None else got_b + own_b
    return got_a + got_b + chunk(z)


def _ring_reduce_scatter(part, sync):
    nmp = lax.axis_size("mp")
    m = lax.axis_index("mp")
    nlo = 2
    nz = nmp // nlo
    z = m // nlo
    lo = m % nlo
    rows = part.shape[0] // nz
    sub = rows // nlo
    halfc = part.shape[1] // 2
    up = [(i, ((i // nlo + 1) % nz) * nlo + i % nlo) for i in range(nmp)]
    down = [(i, ((i // nlo - 1) % nz) * nlo + i % nlo) for i in range(nmp)]
    pa = part[:, :halfc].reshape(nz, rows, halfc)
    pb = part[:, halfc:].reshape(nz, rows, halfc)
    acc = jnp.concatenate(
        [_z_reduce_scatter(pa, z, nz, up, down), _z_reduce_scatter(pb, z, nz, up, down)], axis=1
    )
    mine = lax.dynamic_slice_in_dim(acc, lo * sub, sub, axis=0)
    other = lax.dynamic_slice_in_dim(acc, (1 - lo) * sub, sub, axis=0)
    other, sync = lax.optimization_barrier((other, sync))
    got = lax.ppermute(other.astype(jnp.bfloat16), "mp", [(i, i ^ 1) for i in range(nmp)])
    return (mine + got.astype(jnp.float32)).astype(jnp.bfloat16), sync


def shards(
    tokens,
    cotangent,
    gate_weight,
    up_weight,
    down_master,
    first_moment,
    second_moment,
    anchor,
    outer_momentum,
):
    ndp = lax.axis_size("dp")
    j = lax.axis_index("dp")
    inputs = tokens[0]
    upstream = cotangent[0]
    master = down_master[0]
    down_half = master.astype(jnp.bfloat16)
    ff = master.shape[0]

    assert ndp == 4
    shard = jnp.concatenate([gate_weight[0], up_weight[0], down_half.T], axis=1)
    rows = shard.shape[0]
    half = rows // 2
    from_left = lax.ppermute(shard, "dp", _shift(ndp, 1))
    from_right = lax.ppermute(shard, "dp", _shift(ndp, -1))
    far_a = lax.ppermute(from_left[:half], "dp", _shift(ndp, 1))
    far_b = lax.ppermute(from_right[half:], "dp", _shift(ndp, -1))
    pieces = [
        (j * rows, shard),
        (((j - 1) % ndp) * rows, from_left),
        (((j + 1) % ndp) * rows, from_right),
        (((j + 2) % ndp) * rows, far_a),
        (((j + 2) % ndp) * rows + half, far_b),
    ]

    gu_pre = None
    grad_hidden = None
    weights_full = jnp.zeros((rows * ndp, 2 * ff), jnp.bfloat16)
    for start, piece in pieces:
        size = piece.shape[0]
        xs = lax.dynamic_slice_in_dim(inputs, start, size, axis=1)
        gs = lax.dynamic_slice_in_dim(upstream, start, size, axis=1)
        p1 = jnp.dot(xs, piece[:, : 2 * ff], preferred_element_type=jnp.float32)
        p2 = jnp.dot(gs, piece[:, 2 * ff :], preferred_element_type=jnp.float32)
        gu_pre = p1 if gu_pre is None else gu_pre + p1
        grad_hidden = p2 if grad_hidden is None else grad_hidden + p2
        weights_full = lax.dynamic_update_slice(weights_full, piece[:, : 2 * ff], (start, 0))

    gate_pre = gu_pre[:, :ff]
    up_pre = gu_pre[:, ff:]
    gate_sigmoid = jax.nn.sigmoid(gate_pre)
    active = gate_pre * gate_sigmoid
    hidden = (active * up_pre).astype(jnp.bfloat16)
    grad_up = (grad_hidden * active).astype(jnp.bfloat16)
    grad_gate = (
        grad_hidden * up_pre * gate_sigmoid * (1.0 + gate_pre * (1.0 - gate_sigmoid))
    ).astype(jnp.bfloat16)

    full_grad = lax.dot_general(
        hidden, upstream, (((0,), (0,)), ((), ())), preferred_element_type=jnp.float32
    )
    cols = full_grad.shape[1] // ndp
    grad_down = lax.dynamic_slice_in_dim(full_grad, j * cols, cols, axis=1)
    for s in range(1, ndp):
        blk = lax.dynamic_slice_in_dim(full_grad, ((j + s) % ndp) * cols, cols, axis=1)
        got = lax.ppermute(blk.astype(jnp.bfloat16), "dp", _shift(ndp, s))
        grad_down = grad_down + got.astype(jnp.float32)

    both = jnp.concatenate([grad_gate, grad_up], axis=1)
    partial_sum = lax.dot_general(
        both, weights_full, (((1,), (1,)), ((), ())), preferred_element_type=jnp.float32
    )

    first_new = 0.9 * first_moment[0] + 0.1 * grad_down
    second_new = 0.999 * second_moment[0] + 0.001 * grad_down * grad_down
    adam_step = first_new / bias_one / (jnp.sqrt(second_new / bias_two) + 1e-08) + 0.1 * master
    inner_params = master - 0.001 * adam_step
    drift_local = anchor - inner_params

    nout = lax.axis_size("outer")
    total = drift_local.astype(jnp.bfloat16)
    step = 1
    while step < nout:
        perm = [(i, i ^ step) for i in range(nout)]
        mine = total.astype(jnp.bfloat16)
        total = mine.astype(jnp.float32) + lax.ppermute(mine, "outer", perm).astype(jnp.float32)
        step *= 2
    input_grad, total = _ring_reduce_scatter(partial_sum.astype(jnp.bfloat16), total)
    mean_drift = total / nout
    momentum_out = 0.9 * outer_momentum + mean_drift
    new_params = anchor - 0.7 * (mean_drift + 0.9 * momentum_out)
    return (new_params, first_new[None], second_new[None], momentum_out, input_grad[None])


def solution(mesh):
    return jax.shard_map(
        shards,
        mesh=mesh,
        in_specs=(
            P("outer", "dp", None),
            P("outer", "dp", None),
            P("outer", "dp", "mp"),
            P("outer", "dp", "mp"),
            P("outer", "mp", "dp"),
            P("outer", "mp", "dp"),
            P("outer", "mp", "dp"),
            P("mp", "dp"),
            P("mp", "dp"),
        ),
        out_specs=(
            P("mp", "dp"),
            P("outer", "mp", "dp"),
            P("outer", "mp", "dp"),
            P("mp", "dp"),
            P("outer", ("dp", "mp"), None),
        ),
        check_vma=False,
    )
```

```python
import jax
import jax.numpy as jnp
from jax import lax
from jax.sharding import PartitionSpec as P

bias_one = 1.0 - (0.9**50) ** 2
bias_two = 1.0 - (0.999**50) ** 2


def _shift(n, s):
    return [(i, (i + s) % n) for i in range(n)]


def _z_reduce_scatter(chunks, z, nz, up, down):
    far = nz // 2
    halfc = chunks.shape[2] // 2

    def chunk(c):
        return lax.dynamic_index_in_dim(chunks, c % nz, axis=0, keepdims=False).astype(jnp.float32)

    first = chunk(z + far)
    send_a = first[:, :halfc]
    send_b = first[:, halfc:]
    for r in range(2, far + 2):
        got_a = lax.ppermute(send_a.astype(jnp.bfloat16), "mp", up).astype(jnp.float32)
        got_b = lax.ppermute(send_b.astype(jnp.bfloat16), "mp", down).astype(jnp.float32)
        own_a = chunk(z + far + 1 - r)
        own_b = chunk(z - far - 1 + r)
        if r == 2:
            got_a = jnp.concatenate([got_a, jnp.zeros_like(got_a)], axis=1)
            got_b = jnp.concatenate([jnp.zeros_like(got_b), got_b], axis=1)
        if r <= far:
            send_a = got_a + own_a
            send_b = got_b + own_b
    return own_a + got_a + got_b


def _ring_reduce_scatter(part, sync):
    nmp = lax.axis_size("mp")
    m = lax.axis_index("mp")
    nlo = 2
    nz = nmp // nlo
    z = m // nlo
    lo = m % nlo
    rows = part.shape[0] // nz
    sub = rows // nlo
    halfc = part.shape[1] // 2
    up = [(i, ((i // nlo + 1) % nz) * nlo + i % nlo) for i in range(nmp)]
    down = [(i, ((i // nlo - 1) % nz) * nlo + i % nlo) for i in range(nmp)]
    pa = part[:, :halfc].reshape(nz, rows, halfc)
    pb = part[:, halfc:].reshape(nz, rows, halfc)
    acc = jnp.concatenate(
        [_z_reduce_scatter(pa, z, nz, up, down), _z_reduce_scatter(pb, z, nz, up, down)], axis=1
    )
    mine = lax.dynamic_slice_in_dim(acc, lo * sub, sub, axis=0)
    other = lax.dynamic_slice_in_dim(acc, (1 - lo) * sub, sub, axis=0)
    other, sync = lax.optimization_barrier((other, sync))
    got = lax.ppermute(other.astype(jnp.bfloat16), "mp", [(i, i ^ 1) for i in range(nmp)])
    return (mine + got.astype(jnp.float32)).astype(jnp.bfloat16), sync


def shards(
    tokens,
    cotangent,
    gate_weight,
    up_weight,
    down_master,
    first_moment,
    second_moment,
    anchor,
    outer_momentum,
):
    ndp = lax.axis_size("dp")
    j = lax.axis_index("dp")
    inputs = tokens[0]
    upstream = cotangent[0]
    master = down_master[0]
    down_half = master.astype(jnp.bfloat16)
    ff = master.shape[0]

    assert ndp == 4
    shard = jnp.concatenate([gate_weight[0], up_weight[0], down_half.T], axis=1)
    rows = shard.shape[0]
    half = rows // 2
    from_left = lax.ppermute(shard, "dp", _shift(ndp, 1))
    from_right = lax.ppermute(shard, "dp", _shift(ndp, -1))
    far_a = lax.ppermute(from_left[:half], "dp", _shift(ndp, 1))
    far_b = lax.ppermute(from_right[half:], "dp", _shift(ndp, -1))
    pieces = [
        (j * rows, shard),
        (((j - 1) % ndp) * rows, from_left),
        (((j + 1) % ndp) * rows, from_right),
        (((j + 2) % ndp) * rows, far_a),
        (((j + 2) % ndp) * rows + half, far_b),
    ]

    gu_pre = None
    grad_hidden = None
    weights_full = jnp.zeros((rows * ndp, 2 * ff), jnp.bfloat16)
    for start, piece in pieces:
        size = piece.shape[0]
        xs = lax.dynamic_slice_in_dim(inputs, start, size, axis=1)
        gs = lax.dynamic_slice_in_dim(upstream, start, size, axis=1)
        p1 = jnp.dot(xs, piece[:, : 2 * ff], preferred_element_type=jnp.float32)
        p2 = jnp.dot(gs, piece[:, 2 * ff :], preferred_element_type=jnp.float32)
        gu_pre = p1 if gu_pre is None else gu_pre + p1
        grad_hidden = p2 if grad_hidden is None else grad_hidden + p2
        weights_full = lax.dynamic_update_slice(weights_full, piece[:, : 2 * ff], (start, 0))

    gate_pre = gu_pre[:, :ff]
    up_pre = gu_pre[:, ff:]
    gate_sigmoid = jax.nn.sigmoid(gate_pre)
    active = gate_pre * gate_sigmoid
    hidden = (active * up_pre).astype(jnp.bfloat16)
    grad_up = (grad_hidden * active).astype(jnp.bfloat16)
    grad_gate = (
        grad_hidden * up_pre * gate_sigmoid * (1.0 + gate_pre * (1.0 - gate_sigmoid))
    ).astype(jnp.bfloat16)

    full_grad = lax.dot_general(
        hidden, upstream, (((0,), (0,)), ((), ())), preferred_element_type=jnp.float32
    )
    cols = full_grad.shape[1] // ndp
    grad_down = lax.dynamic_slice_in_dim(full_grad, j * cols, cols, axis=1)
    sent = full_grad.astype(jnp.bfloat16)
    for s in range(1, ndp):
        blk = lax.dynamic_slice_in_dim(sent, ((j + s) % ndp) * cols, cols, axis=1)
        got = lax.ppermute(blk, "dp", _shift(ndp, s))
        grad_down = grad_down + got.astype(jnp.float32)

    both = jnp.concatenate([grad_gate, grad_up], axis=1)
    partial_sum = lax.dot_general(
        both, weights_full, (((1,), (1,)), ((), ())), preferred_element_type=jnp.float32
    )

    first_new = 0.9 * first_moment[0] + 0.1 * grad_down
    second_new = 0.999 * second_moment[0] + 0.001 * grad_down * grad_down
    adam_step = first_new / bias_one / (jnp.sqrt(second_new / bias_two) + 1e-08) + 0.1 * master
    inner_params = master - 0.001 * adam_step
    drift_local = anchor - inner_params

    nout = lax.axis_size("outer")
    total = drift_local.astype(jnp.bfloat16)
    step = 1
    while step < nout:
        perm = [(i, i ^ step) for i in range(nout)]
        mine = total.astype(jnp.bfloat16)
        total = mine.astype(jnp.float32) + lax.ppermute(mine, "outer", perm).astype(jnp.float32)
        step *= 2
    input_grad, total = _ring_reduce_scatter(partial_sum.astype(jnp.bfloat16), total)
    mean_drift = total / nout
    momentum_out = 0.9 * outer_momentum + mean_drift
    new_params = anchor - 0.7 * (mean_drift + 0.9 * momentum_out)
    return (new_params, first_new[None], second_new[None], momentum_out, input_grad[None])


def solution(mesh):
    return jax.shard_map(
        shards,
        mesh=mesh,
        in_specs=(
            P("outer", "dp", None),
            P("outer", "dp", None),
            P("outer", "dp", "mp"),
            P("outer", "dp", "mp"),
            P("outer", "mp", "dp"),
            P("outer", "mp", "dp"),
            P("outer", "mp", "dp"),
            P("mp", "dp"),
            P("mp", "dp"),
        ),
        out_specs=(
            P("mp", "dp"),
            P("outer", "mp", "dp"),
            P("outer", "mp", "dp"),
            P("mp", "dp"),
            P("outer", ("dp", "mp"), None),
        ),
        check_vma=False,
    )
```

```python
import jax
import jax.numpy as jnp
from jax import lax
from jax.sharding import PartitionSpec as P

bias_one = 1.0 - (0.9**50) ** 2
bias_two = 1.0 - (0.999**50) ** 2


def _shift(n, s):
    return [(i, (i + s) % n) for i in range(n)]


def _z_reduce_scatter(chunks, z, nz, up, down):
    far = nz // 2
    halfc = chunks.shape[2] // 2

    def chunk(c):
        return lax.dynamic_index_in_dim(chunks, c % nz, axis=0, keepdims=False).astype(jnp.float32)

    first = chunk(z + far)
    send_a = first[:, :halfc]
    send_b = first[:, halfc:]
    for r in range(2, far + 2):
        got_a = lax.ppermute(send_a.astype(jnp.bfloat16), "mp", up).astype(jnp.float32)
        got_b = lax.ppermute(send_b.astype(jnp.bfloat16), "mp", down).astype(jnp.float32)
        own_a = chunk(z + far + 1 - r)
        own_b = chunk(z - far - 1 + r)
        if r == 2:
            got_a = jnp.concatenate([got_a, jnp.zeros_like(got_a)], axis=1)
            got_b = jnp.concatenate([jnp.zeros_like(got_b), got_b], axis=1)
        if r <= far:
            send_a = got_a + own_a
            send_b = got_b + own_b
    return own_a + got_a + got_b


def _ring_reduce_scatter(part, sync):
    nmp = lax.axis_size("mp")
    m = lax.axis_index("mp")
    nlo = 2
    nz = nmp // nlo
    z = m // nlo
    lo = m % nlo
    rows = part.shape[0] // nz
    sub = rows // nlo
    halfc = part.shape[1] // 2
    up = [(i, ((i // nlo + 1) % nz) * nlo + i % nlo) for i in range(nmp)]
    down = [(i, ((i // nlo - 1) % nz) * nlo + i % nlo) for i in range(nmp)]
    pa = part[:, :halfc].reshape(nz, rows, halfc)
    pb = part[:, halfc:].reshape(nz, rows, halfc)
    acc = jnp.concatenate(
        [_z_reduce_scatter(pa, z, nz, up, down), _z_reduce_scatter(pb, z, nz, up, down)], axis=1
    )
    mine = lax.dynamic_slice_in_dim(acc, lo * sub, sub, axis=0)
    other = lax.dynamic_slice_in_dim(acc, (1 - lo) * sub, sub, axis=0)
    other, sync = lax.optimization_barrier((other, sync))
    got = lax.ppermute(other.astype(jnp.bfloat16), "mp", [(i, i ^ 1) for i in range(nmp)])
    return (mine + got.astype(jnp.float32)).astype(jnp.bfloat16), sync


def shards(
    tokens,
    cotangent,
    gate_weight,
    up_weight,
    down_master,
    first_moment,
    second_moment,
    anchor,
    outer_momentum,
):
    ndp = lax.axis_size("dp")
    j = lax.axis_index("dp")
    inputs = tokens[0]
    upstream = cotangent[0]
    master = down_master[0]
    down_half = master.astype(jnp.bfloat16)
    ff = master.shape[0]

    assert ndp == 4
    shard = jnp.concatenate([gate_weight[0], up_weight[0], down_half.T], axis=1)
    rows = shard.shape[0]
    half = rows // 2
    left_a = lax.ppermute(shard[:half], "dp", _shift(ndp, 1))
    right_b = lax.ppermute(shard[half:], "dp", _shift(ndp, -1))
    left_b = lax.ppermute(shard[half:], "dp", _shift(ndp, 1))
    right_a = lax.ppermute(shard[:half], "dp", _shift(ndp, -1))
    far_a = lax.ppermute(left_a, "dp", _shift(ndp, 1))
    far_b = lax.ppermute(right_b, "dp", _shift(ndp, -1))
    pieces = [
        (j * rows, shard),
        (((j - 1) % ndp) * rows, left_a),
        (((j - 1) % ndp) * rows + half, left_b),
        (((j + 1) % ndp) * rows, right_a),
        (((j + 1) % ndp) * rows + half, right_b),
        (((j + 2) % ndp) * rows, far_a),
        (((j + 2) % ndp) * rows + half, far_b),
    ]

    gu_pre = None
    grad_hidden = None
    weights_full = jnp.zeros((rows * ndp, 2 * ff), jnp.bfloat16)
    for start, piece in pieces:
        size = piece.shape[0]
        xs = lax.dynamic_slice_in_dim(inputs, start, size, axis=1)
        gs = lax.dynamic_slice_in_dim(upstream, start, size, axis=1)
        p1 = jnp.dot(xs, piece[:, : 2 * ff], preferred_element_type=jnp.float32)
        p2 = jnp.dot(gs, piece[:, 2 * ff :], preferred_element_type=jnp.float32)
        gu_pre = p1 if gu_pre is None else gu_pre + p1
        grad_hidden = p2 if grad_hidden is None else grad_hidden + p2
        weights_full = lax.dynamic_update_slice(weights_full, piece[:, : 2 * ff], (start, 0))

    gate_pre = gu_pre[:, :ff]
    up_pre = gu_pre[:, ff:]
    gate_sigmoid = jax.nn.sigmoid(gate_pre)
    active = gate_pre * gate_sigmoid
    hidden = (active * up_pre).astype(jnp.bfloat16)
    grad_up = (grad_hidden * active).astype(jnp.bfloat16)
    grad_gate = (
        grad_hidden * up_pre * gate_sigmoid * (1.0 + gate_pre * (1.0 - gate_sigmoid))
    ).astype(jnp.bfloat16)

    full_grad = lax.dot_general(
        hidden, upstream, (((0,), (0,)), ((), ())), preferred_element_type=jnp.float32
    )
    cols = full_grad.shape[1] // ndp
    grad_down = lax.dynamic_slice_in_dim(full_grad, j * cols, cols, axis=1)
    for s in range(1, ndp):
        blk = lax.dynamic_slice_in_dim(full_grad, ((j + s) % ndp) * cols, cols, axis=1)
        got = lax.ppermute(blk.astype(jnp.bfloat16), "dp", _shift(ndp, s))
        grad_down = grad_down + got.astype(jnp.float32)

    both = jnp.concatenate([grad_gate, grad_up], axis=1)
    partial_sum = lax.dot_general(
        both, weights_full, (((1,), (1,)), ((), ())), preferred_element_type=jnp.float32
    )

    first_new = 0.9 * first_moment[0] + 0.1 * grad_down
    second_new = 0.999 * second_moment[0] + 0.001 * grad_down * grad_down
    adam_step = first_new / bias_one / (jnp.sqrt(second_new / bias_two) + 1e-08) + 0.1 * master
    inner_params = master - 0.001 * adam_step
    drift_local = anchor - inner_params

    nout = lax.axis_size("outer")
    total = drift_local.astype(jnp.bfloat16)
    step = 1
    while step < nout:
        perm = [(i, i ^ step) for i in range(nout)]
        mine = total.astype(jnp.bfloat16)
        total = mine.astype(jnp.float32) + lax.ppermute(mine, "outer", perm).astype(jnp.float32)
        step *= 2
    input_grad, total = _ring_reduce_scatter(partial_sum.astype(jnp.bfloat16), total)
    mean_drift = total / nout
    momentum_out = 0.9 * outer_momentum + mean_drift
    new_params = anchor - 0.7 * (mean_drift + 0.9 * momentum_out)
    return (new_params, first_new[None], second_new[None], momentum_out, input_grad[None])


def solution(mesh):
    return jax.shard_map(
        shards,
        mesh=mesh,
        in_specs=(
            P("outer", "dp", None),
            P("outer", "dp", None),
            P("outer", "dp", "mp"),
            P("outer", "dp", "mp"),
            P("outer", "mp", "dp"),
            P("outer", "mp", "dp"),
            P("outer", "mp", "dp"),
            P("mp", "dp"),
            P("mp", "dp"),
        ),
        out_specs=(
            P("mp", "dp"),
            P("outer", "mp", "dp"),
            P("outer", "mp", "dp"),
            P("mp", "dp"),
            P("outer", ("dp", "mp"), None),
        ),
        check_vma=False,
    )
```
